512 devices in a mesh: tm: 16 (over z, core), pairs: 32 (over y, x).
Axes of the slice: x: 4, y: 8, z: 8, core: 2. Of those that a mesh axis runs over, the one named last changes fastest.
Arguments:
- record: bfloat16 [128, 3, 16, 4096], P('pairs', None, 'tm')
- requested: int32 [32, 32, 2], replicated, may hold values from 0 to 3, as said below
- partners: int32 [32, 12, 48], P('pairs'), may hold values from 0 to 63
- codes: int32 [32, 12, 48], P('pairs'), may hold values from 0 to 2
- counts: int32 [32, 12], P('pairs'), may hold values from 1 to 48, as said below
Outputs:
- stacks: float32 [32, 576, 1024], P('pairs', 'tm')
The draws below stay inside these ranges and needn't reach their ends.
Inputs may be any that keep to these rules, and one draw needn't show every extreme that they name: requested[e, d] holds 2 different local station indices of device d, meaning stations d * 4 + requested[e, d, i]. `partners`: slot k stands for the station requested[e, k // 2, k % 2]. Slots at and after counts[e, j] are unused; on some device every owned trace has 48 live slots.
All inputs are finite; a program needn't handle non-finite values.
Results may differ from the reference program's by a relative error of at most 0.0037.
Values may be sent and summed in bfloat16 or wider, within the bound.
No kernel may reach another device: no remote copies, remote signals or barrier semaphores. Data moves between devices by JAX's collectives and lax.ppermute only.
A program may use at most 64 MiB of HBM per device.

```python
import math
import jax
import jax.numpy as jnp
from jax import lax

S_DEV = 4
PER = 48
CAP = 2
WIN = 4096
LAGS = 1024
OWNERS = 32
STATIONS = 128
WINDOWS = 16


def draw_record(key, part):
    noise_key, scale_key = jax.random.split(key, 2)
    shape_all = (STATIONS, 3, WINDOWS, WIN)
    shape_amp = (STATIONS, 3, WINDOWS, 1)
    noise_part = jnp.clip(jax.random.normal(noise_key, shape_all, jnp.float32), -6.0, 6.0)
    scales = jnp.exp(jax.random.uniform(scale_key, shape_amp, jnp.float32, 0.0, math.log(10.0)))
    return (noise_part * scales).astype(jnp.bfloat16)


def draw_requested(key, part):
    scores = jax.random.randint(key, (OWNERS, OWNERS, S_DEV), 0, 1 << 20)
    scores = scores * S_DEV + jnp.arange(S_DEV, dtype=jnp.int32)[None, None, :]
    order = jnp.argsort(scores, axis=-1, stable=True)
    return order[..., :CAP].astype(jnp.int32)


def draw_counts(key, part):
    base_key, cut_key, full_key = jax.random.split(key, 3)
    base_load = jax.random.randint(base_key, (OWNERS, 1), max(PER // 4, 1), PER + 1)
    cut_rows = jax.random.randint(cut_key, (OWNERS, 3 * S_DEV), 0, PER + 1) % (base_load // 4 + 1)
    full_owner = jax.random.randint(full_key, (), 0, OWNERS)
    rows_owner = jnp.arange(OWNERS, dtype=jnp.int32)[:, None]
    result = jnp.where(rows_owner == full_owner, PER, base_load - cut_rows)
    return result.astype(jnp.int32)


def plant(array, stream_key, least, top_value):
    shape = array.shape
    place = [jax.random.randint(jax.random.fold_in(stream_key, axis), (), 0, shape[axis]) for axis in range(len(shape))]
    array = array.at[tuple(place)].set(least)
    longest = shape.index(max(shape))
    place[longest] = (place[longest] + 1) % shape[longest]
    return array.at[tuple(place)].set(top_value)


def setup_inputs(seed: int = 0) -> dict:
    keys = jax.random.split(jax.random.key(seed), 6)
    return {
        "record": draw_record(jax.random.fold_in(keys[5], 71), 0),
        "requested": draw_requested(jax.random.fold_in(keys[5], 71), 0),
        "partners": plant(jax.random.randint(keys[2], (OWNERS, 3 * S_DEV, PER), 0, OWNERS * CAP), jax.random.fold_in(keys[2], 1), 0, (OWNERS * CAP) - 1).astype(jnp.int32),
        "codes": plant(jax.random.randint(keys[3], (OWNERS, 3 * S_DEV, PER), 0, 3), jax.random.fold_in(keys[3], 1), 0, 2).astype(jnp.int32),
        "counts": draw_counts(jax.random.fold_in(keys[5], 71), 0),
    }


def reference(record, requested, partners, codes, counts):
    values = record.astype(jnp.float32)
    values = values - lax.optimization_barrier(jnp.mean(values, axis=-1, keepdims=True))
    power_mean = lax.optimization_barrier(jnp.mean(values * values, axis=-1, keepdims=True))
    whitened = (values * lax.rsqrt(power_mean + 1e-06)).astype(jnp.bfloat16)
    fft_len = 2 * WIN
    half_lag = LAGS // 2
    spectra = jnp.fft.rfft(whitened.astype(jnp.float32), n=fft_len, axis=-1)
    flat_spectra = spectra.reshape(STATIONS * 3, WINDOWS, spectra.shape[-1])

    def per_owner(owner_index):
        own_spec = lax.dynamic_slice_in_dim(flat_spectra, owner_index * (S_DEV * 3), S_DEV * 3, 0)
        asked_table = lax.dynamic_index_in_dim(requested, owner_index, axis=0, keepdims=False)
        station_of = (asked_table + jnp.arange(OWNERS, dtype=jnp.int32)[:, None] * S_DEV).reshape(-1)
        slot_ids = lax.dynamic_index_in_dim(partners, owner_index, axis=0, keepdims=False)
        comp_ids = lax.dynamic_index_in_dim(codes, owner_index, axis=0, keepdims=False)
        live_count = lax.dynamic_index_in_dim(counts, owner_index, axis=0, keepdims=False)
        row_ids = (station_of[slot_ids] * 3 + comp_ids).astype(jnp.int32)

        def per_trace(operands):
            own_row, trace_rows, live_n = operands
            partner_spec = flat_spectra[trace_rows]
            cross_spec = lax.optimization_barrier(jnp.sum(jnp.conj(partner_spec) * own_row[None], axis=1))
            lagged = jnp.fft.irfft(cross_spec, n=fft_len, axis=-1)
            picked = jnp.concatenate([lagged[:, fft_len - half_lag:], lagged[:, :LAGS - half_lag]], axis=1)
            live_rows = (jnp.arange(PER, dtype=jnp.int32) < live_n)[:, None]
            return jnp.where(live_rows, picked, 0.0)
        return lax.map(per_trace, (own_spec, row_ids, live_count))
    stacked = lax.map(per_owner, jnp.arange(OWNERS, dtype=jnp.int32))
    stacked = stacked.reshape(OWNERS, 3 * S_DEV * PER, LAGS)
    return (stacked / jnp.sqrt(jnp.float32(WIN * WINDOWS))).astype(jnp.float32)
```

```python
import math

import jax
import jax.numpy as jnp
from jax import lax
from jax.experimental import pallas as pl
from jax.experimental.pallas import tpu as pltpu
from jax.sharding import PartitionSpec as P

LAGS = 1024
BLK = 256
LANE = 128


def normalize(traces):
    values = traces.astype(jnp.float32)
    values = values - jnp.mean(values, axis=-1, keepdims=True)
    power_mean = jnp.mean(values * values, axis=-1, keepdims=True)
    return (values * lax.rsqrt(power_mean + 1e-06)).astype(jnp.bfloat16)


def flip_lanes(rows):
    shape = rows.shape
    grouped = rows.reshape(shape[:-1] + (shape[-1] // LANE, LANE))
    return grouped[..., ::-1].reshape(shape)


def corr_kernel(src_ref, p_ref, o_ref, *, win, scale):
    rows = p_ref.shape[1]
    span = src_ref.shape[2]
    m_blocks = win // BLK
    o_blocks = LAGS // BLK
    d_blocks = m_blocks + o_blocks - 1
    width = BLK * (d_blocks - 1) + BLK + LANE
    wide = jnp.broadcast_to(src_ref[0], (LANE, span))
    hank = pltpu.roll(wide, span - (LANE - 1), 1, stride=1, stride_axis=0)
    hank = hank[:, :width].astype(jnp.bfloat16)
    acc = [jnp.zeros((rows, BLK), jnp.float32) for _ in range(o_blocks)]
    for d in range(d_blocks):
        rhs = jnp.concatenate(
            [hank[:, BLK * d: BLK * d + BLK], hank[:, BLK * d + LANE: BLK * d + LANE + BLK]], axis=0
        )
        lags = [o for o in range(o_blocks) if 0 <= d - o < m_blocks]
        lhs = jnp.concatenate([p_ref[0, :, BLK * (d - o): BLK * (d - o) + BLK] for o in lags], axis=0)
        res = jnp.dot(lhs, rhs, preferred_element_type=jnp.float32)
        for k, o in enumerate(lags):
            acc[o] = acc[o] + res[rows * k: rows * (k + 1)]
    o_ref[0] = jnp.concatenate(acc, axis=1) * scale


def correlate(src, partner_rows, scale):
    traces, rows, win = partner_rows.shape
    span = src.shape[-1]
    flops = 2 * traces * rows * win * LAGS
    return pl.pallas_call(
        lambda s, p, o: corr_kernel(s, p, o, win=win, scale=scale),
        grid=(traces,),
        in_specs=[
            pl.BlockSpec((1, 1, span), lambda j: (j, 0, 0)),
            pl.BlockSpec((1, rows, win), lambda j: (j, 0, 0)),
        ],
        out_specs=pl.BlockSpec((1, rows, LAGS), lambda j: (j, 0, 0)),
        out_shape=jax.ShapeDtypeStruct((traces, rows, LAGS), jnp.float32),
        cost_estimate=pl.CostEstimate(
            flops=flops, transcendentals=0,
            bytes_accessed=traces * (rows * win * 2 + span * 4 + rows * LAGS * 4),
        ),
        name="xcorr",
    )(src.reshape(traces, 1, span), partner_rows)


def shards(record, requested, partners, codes, counts):
    whitened = normalize(record)
    local_stations, comp_count, window_count, window_len = whitened.shape
    owners = lax.axis_size("pairs")
    tm_count = lax.axis_size("tm")
    capacity = requested.shape[2]
    per_trace = partners.shape[2]
    trace_count = local_stations * comp_count
    own_index = lax.axis_index("pairs")
    slot_ids = partners[0]
    comp_ids = codes[0]
    everyone = lax.all_gather(flip_lanes(whitened), "pairs", axis=0, tiled=True)
    trace_pool = everyone.reshape(owners * local_stations * comp_count, window_count * window_len)
    asked_table = lax.dynamic_index_in_dim(requested, own_index, axis=0, keepdims=False)
    station_of = (
        asked_table + jnp.arange(owners, dtype=jnp.int32)[:, None] * local_stations
    ).reshape(-1)
    matches = slot_ids[:, :, None] == jnp.arange(owners * capacity, dtype=jnp.int32)[None, None, :]
    stations = jnp.sum(jnp.where(matches, station_of[None, None, :], 0), axis=-1)
    row_ids = stations * comp_count + comp_ids
    picked = jnp.take(trace_pool, row_ids.reshape(-1), axis=0)
    live_rows = jnp.arange(per_trace, dtype=jnp.int32)[None, :] < counts[0][:, None]
    picked = jnp.where(live_rows.reshape(-1)[:, None], picked, jnp.zeros((), jnp.bfloat16))
    picked = picked.reshape(trace_count, per_trace, window_len)
    half = LAGS // 2
    own = whitened.reshape(trace_count, window_len).astype(jnp.float32)
    span = ((window_len + LAGS + LANE - 1) // LANE) * LANE
    src = jnp.pad(own, ((0, 0), (half, span - window_len - half)))
    total_windows = window_count * tm_count
    scale = 1.0 / math.sqrt(window_len * total_windows)
    lagged = correlate(src, picked, scale)
    lagged = lagged.reshape(tm_count, trace_count * per_trace // tm_count, LAGS)
    out = lax.psum_scatter(lagged, "tm", scatter_dimension=0, tiled=True)
    return out.reshape(1, trace_count * per_trace // tm_count, LAGS)


def solution(mesh):
    return jax.shard_map(
        shards,
        mesh=mesh,
        in_specs=(
            P("pairs", None, "tm", None),
            P(),
            P("pairs", None, None),
            P("pairs", None, None),
            P("pairs", None),
        ),
        out_specs=P("pairs", "tm", None),
        check_vma=False,
    )
```

```python
import math

import jax
import jax.numpy as jnp
from jax import lax
from jax.experimental import pallas as pl
from jax.experimental.pallas import tpu as pltpu
from jax.sharding import PartitionSpec as P

LAGS = 1024
BLK = 256
LANE = 128


def normalize(traces):
    values = traces.astype(jnp.float32)
    values = values - jnp.mean(values, axis=-1, keepdims=True)
    power_mean = jnp.mean(values * values, axis=-1, keepdims=True)
    return (values * lax.rsqrt(power_mean + 1e-06)).astype(jnp.bfloat16)


def flip_lanes(rows):
    shape = rows.shape
    grouped = rows.reshape(shape[:-1] + (shape[-1] // LANE, LANE))
    return grouped[..., ::-1].reshape(shape)


def corr_kernel(src_ref, p_ref, o_ref, *, win, scale):
    rows = p_ref.shape[1]
    span = src_ref.shape[2]
    m_blocks = win // BLK
    o_blocks = LAGS // BLK
    d_blocks = m_blocks + o_blocks - 1
    width = BLK * (d_blocks - 1) + BLK + LANE
    wide = jnp.broadcast_to(src_ref[0], (LANE, span))
    hank = pltpu.roll(wide, span - (LANE - 1), 1, stride=1, stride_axis=0)
    hank = hank[:, :width].astype(jnp.bfloat16)
    acc = [jnp.zeros((rows, BLK), jnp.float32) for _ in range(o_blocks)]
    for d in range(d_blocks):
        rhs = jnp.concatenate(
            [hank[:, BLK * d: BLK * d + BLK], hank[:, BLK * d + LANE: BLK * d + LANE + BLK]], axis=0
        )
        lags = [o for o in range(o_blocks) if 0 <= d - o < m_blocks]
        lhs = jnp.concatenate([p_ref[0, :, BLK * (d - o): BLK * (d - o) + BLK] for o in lags], axis=0)
        res = jnp.dot(lhs, rhs, preferred_element_type=jnp.float32)
        for k, o in enumerate(lags):
            acc[o] = acc[o] + res[rows * k: rows * (k + 1)]
    o_ref[0] = jnp.concatenate(acc, axis=1) * scale


def correlate(src, partner_rows, scale):
    traces, rows, win = partner_rows.shape
    span = src.shape[-1]
    flops = 2 * traces * rows * win * LAGS
    return pl.pallas_call(
        lambda s, p, o: corr_kernel(s, p, o, win=win, scale=scale),
        grid=(traces,),
        in_specs=[
            pl.BlockSpec((1, 1, span), lambda j: (j, 0, 0)),
            pl.BlockSpec((1, rows, win), lambda j: (j, 0, 0)),
        ],
        out_specs=pl.BlockSpec((1, rows, LAGS), lambda j: (j, 0, 0)),
        out_shape=jax.ShapeDtypeStruct((traces, rows, LAGS), jnp.float32),
        cost_estimate=pl.CostEstimate(
            flops=flops, transcendentals=0,
            bytes_accessed=traces * (rows * win * 2 + span * 4 + rows * LAGS * 4),
        ),
        name="xcorr",
    )(src.reshape(traces, 1, span), partner_rows)


def shards(record, requested, partners, codes, counts):
    whitened = normalize(record)
    local_stations, comp_count, window_count, window_len = whitened.shape
    owners = lax.axis_size("pairs")
    tm_count = lax.axis_size("tm")
    capacity = requested.shape[2]
    per_trace = partners.shape[2]
    trace_count = local_stations * comp_count
    own_index = lax.axis_index("pairs")
    slot_ids = partners[0]
    comp_ids = codes[0]
    mine = flip_lanes(whitened).reshape(local_stations, comp_count * window_count * window_len)
    asked_of_me = lax.dynamic_index_in_dim(requested, own_index, axis=1, keepdims=False)
    outgoing = jnp.take(mine, asked_of_me.reshape(-1), axis=0)
    outgoing = outgoing.reshape(owners, capacity * comp_count, window_count * window_len)
    arrived = lax.all_to_all(outgoing, "pairs", 0, 0, tiled=True)
    trace_pool = arrived.reshape(owners * capacity * comp_count, window_count * window_len)
    row_ids = slot_ids * comp_count + comp_ids
    picked = jnp.take(trace_pool, row_ids.reshape(-1), axis=0)
    live_rows = jnp.arange(per_trace, dtype=jnp.int32)[None, :] < counts[0][:, None]
    picked = jnp.where(live_rows.reshape(-1)[:, None], picked, jnp.zeros((), jnp.bfloat16))
    picked = picked.reshape(trace_count, per_trace, window_len)
    half = LAGS // 2
    own = whitened.reshape(trace_count, window_len).astype(jnp.float32)
    span = ((window_len + LAGS + LANE - 1) // LANE) * LANE
    src = jnp.pad(own, ((0, 0), (half, span - window_len - half)))
    total_windows = window_count * tm_count
    scale = 1.0 / math.sqrt(window_len * total_windows)
    lagged = correlate(src, picked, scale)
    lagged = lagged.reshape(tm_count, trace_count * per_trace // tm_count, LAGS)
    out = lax.psum_scatter(lagged, "tm", scatter_dimension=0, tiled=True)
    return out.reshape(1, trace_count * per_trace // tm_count, LAGS)


def solution(mesh):
    return jax.shard_map(
        shards,
        mesh=mesh,
        in_specs=(
            P("pairs", None, "tm", None),
            P(),
            P("pairs", None, None),
            P("pairs", None, None),
            P("pairs", None),
        ),
        out_specs=P("pairs", "tm", None),
        check_vma=False,
    )
```

```python
import math

import jax
import jax.numpy as jnp
from jax import lax
from jax.experimental import pallas as pl
from jax.experimental.pallas import tpu as pltpu
from jax.sharding import PartitionSpec as P

LAGS = 1024
BLK = 256
LANE = 128


def normalize(traces):
    values = traces.astype(jnp.float32)
    values = values - jnp.mean(values, axis=-1, keepdims=True)
    power_mean = jnp.mean(values * values, axis=-1, keepdims=True)
    return (values * lax.rsqrt(power_mean + 1e-06)).astype(jnp.bfloat16)


def flip_lanes(rows):
    shape = rows.shape
    grouped = rows.reshape(shape[:-1] + (shape[-1] // LANE, LANE))
    return grouped[..., ::-1].reshape(shape)


def corr_kernel(src_ref, p_ref, o_ref, *, win, scale):
    rows = p_ref.shape[1]
    span = src_ref.shape[2]
    m_blocks = win // BLK
    o_blocks = LAGS // BLK
    d_blocks = m_blocks + o_blocks - 1
    width = BLK * (d_blocks - 1) + BLK + LANE
    wide = jnp.broadcast_to(src_ref[0], (LANE, span))
    hank = pltpu.roll(wide, span - (LANE - 1), 1, stride=1, stride_axis=0)
    hank = hank[:, :width].astype(jnp.bfloat16)
    acc = [jnp.zeros((rows, BLK), jnp.float32) for _ in range(o_blocks)]
    for d in range(d_blocks):
        rhs = jnp.concatenate(
            [hank[:, BLK * d: BLK * d + BLK], hank[:, BLK * d + LANE: BLK * d + LANE + BLK]], axis=0
        )
        lags = [o for o in range(o_blocks) if 0 <= d - o < m_blocks]
        lhs = jnp.concatenate([p_ref[0, :, BLK * (d - o): BLK * (d - o) + BLK] for o in lags], axis=0)
        res = jnp.dot(lhs, rhs, preferred_element_type=jnp.float32)
        for k, o in enumerate(lags):
            acc[o] = acc[o] + res[rows * k: rows * (k + 1)]
    o_ref[0] = (jnp.concatenate(acc, axis=1) * scale).astype(o_ref.dtype)


def correlate(src, partner_rows, scale):
    traces, rows, win = partner_rows.shape
    span = src.shape[-1]
    flops = 2 * traces * rows * win * LAGS
    return pl.pallas_call(
        lambda s, p, o: corr_kernel(s, p, o, win=win, scale=scale),
        grid=(traces,),
        in_specs=[
            pl.BlockSpec((1, 1, span), lambda j: (j, 0, 0)),
            pl.BlockSpec((1, rows, win), lambda j: (j, 0, 0)),
        ],
        out_specs=pl.BlockSpec((1, rows, LAGS), lambda j: (j, 0, 0)),
        out_shape=jax.ShapeDtypeStruct((traces, rows, LAGS), jnp.bfloat16),
        cost_estimate=pl.CostEstimate(
            flops=flops, transcendentals=0,
            bytes_accessed=traces * (rows * win * 2 + span * 4 + rows * LAGS * 2),
        ),
        name="xcorr",
    )(src.reshape(traces, 1, span), partner_rows)


def shards(record, requested, partners, codes, counts):
    whitened = normalize(record)
    local_stations, comp_count, window_count, window_len = whitened.shape
    owners = lax.axis_size("pairs")
    tm_count = lax.axis_size("tm")
    capacity = requested.shape[2]
    per_trace = partners.shape[2]
    trace_count = local_stations * comp_count
    own_index = lax.axis_index("pairs")
    slot_ids = partners[0]
    comp_ids = codes[0]
    mine = flip_lanes(whitened).reshape(local_stations, comp_count * window_count * window_len)
    asked_of_me = lax.dynamic_index_in_dim(requested, own_index, axis=1, keepdims=False)
    outgoing = jnp.take(mine, asked_of_me.reshape(-1), axis=0)
    outgoing = outgoing.reshape(owners, capacity * comp_count, window_count * window_len)
    arrived = lax.all_to_all(outgoing, "pairs", 0, 0, tiled=True)
    trace_pool = arrived.reshape(owners * capacity * comp_count, window_count * window_len)
    row_ids = slot_ids * comp_count + comp_ids
    picked = jnp.take(trace_pool, row_ids.reshape(-1), axis=0)
    live_rows = jnp.arange(per_trace, dtype=jnp.int32)[None, :] < counts[0][:, None]
    picked = jnp.where(live_rows.reshape(-1)[:, None], picked, jnp.zeros((), jnp.bfloat16))
    picked = picked.reshape(trace_count, per_trace, window_len)
    half = LAGS // 2
    own = whitened.reshape(trace_count, window_len).astype(jnp.float32)
    span = ((window_len + LAGS + LANE - 1) // LANE) * LANE
    src = jnp.pad(own, ((0, 0), (half, span - window_len - half)))
    total_windows = window_count * tm_count
    scale = 1.0 / math.sqrt(window_len * total_windows)
    lagged = correlate(src, picked, scale)
    lagged = lagged.reshape(tm_count, trace_count * per_trace // tm_count, LAGS)
    arrived_sums = lax.all_to_all(lagged, "tm", 0, 0, tiled=True)
    out = jnp.sum(arrived_sums.astype(jnp.float32), axis=0, keepdims=True)
    return out


def solution(mesh):
    return jax.shard_map(
        shards,
        mesh=mesh,
        in_specs=(
            P("pairs", None, "tm", None),
            P(),
            P("pairs", None, None),
            P("pairs", None, None),
            P("pairs", None),
        ),
        out_specs=P("pairs", "tm", None),
        check_vma=False,
    )
```

```python
import math

import jax
import jax.numpy as jnp
from jax import lax
from jax.experimental import pallas as pl
from jax.experimental.pallas import tpu as pltpu
from jax.sharding import PartitionSpec as P

LAGS = 1024
BLK = 256
LANE = 128


def normalize(traces):
    values = traces.astype(jnp.float32)
    values = values - jnp.mean(values, axis=-1, keepdims=True)
    power_mean = jnp.mean(values * values, axis=-1, keepdims=True)
    return (values * lax.rsqrt(power_mean + 1e-06)).astype(jnp.bfloat16)


def flip_lanes(rows):
    shape = rows.shape
    grouped = rows.reshape(shape[:-1] + (shape[-1] // LANE, LANE))
    return grouped[..., ::-1].reshape(shape)


def corr_kernel(src_ref, p_ref, o_ref, *, win, scale):
    rows = p_ref.shape[1]
    span = src_ref.shape[2]
    m_blocks = win // BLK
    o_blocks = LAGS // BLK
    d_blocks = m_blocks + o_blocks - 1
    width = BLK * (d_blocks - 1) + BLK + LANE
    wide = jnp.broadcast_to(src_ref[0], (LANE, span))
    hank = pltpu.roll(wide, span - (LANE - 1), 1, stride=1, stride_axis=0)
    hank = hank[:, :width].astype(jnp.bfloat16)
    acc = [jnp.zeros((rows, BLK), jnp.float32) for _ in range(o_blocks)]
    for d in range(d_blocks):
        rhs = jnp.concatenate(
            [hank[:, BLK * d: BLK * d + BLK], hank[:, BLK * d + LANE: BLK * d + LANE + BLK]], axis=0
        )
        lags = [o for o in range(o_blocks) if 0 <= d - o < m_blocks]
        lhs = jnp.concatenate([p_ref[0, :, BLK * (d - o): BLK * (d - o) + BLK] for o in lags], axis=0)
        res = jnp.dot(lhs, rhs, preferred_element_type=jnp.float32)
        for k, o in enumerate(lags):
            acc[o] = acc[o] + res[rows * k: rows * (k + 1)]
    o_ref[0] = jnp.concatenate(acc, axis=1) * scale


def correlate(src, partner_rows, scale):
    traces, rows, win = partner_rows.shape
    span = src.shape[-1]
    flops = 2 * traces * rows * win * LAGS
    return pl.pallas_call(
        lambda s, p, o: corr_kernel(s, p, o, win=win, scale=scale),
        grid=(traces,),
        in_specs=[
            pl.BlockSpec((1, 1, span), lambda j: (j, 0, 0)),
            pl.BlockSpec((1, rows, win), lambda j: (j, 0, 0)),
        ],
        out_specs=pl.BlockSpec((1, rows, LAGS), lambda j: (j, 0, 0)),
        out_shape=jax.ShapeDtypeStruct((traces, rows, LAGS), jnp.float32),
        cost_estimate=pl.CostEstimate(
            flops=flops, transcendentals=0,
            bytes_accessed=traces * (rows * win * 2 + span * 4 + rows * LAGS * 4),
        ),
        name="xcorr",
    )(src.reshape(traces, 1, span), partner_rows)


def shards(record, requested, partners, codes, counts):
    whitened = normalize(record)
    local_stations, comp_count, window_count, window_len = whitened.shape
    owners = lax.axis_size("pairs")
    chips = lax.axis_size("z")
    cores = lax.axis_size("c")
    tm_count = chips * cores
    capacity = requested.shape[2]
    per_trace = partners.shape[2]
    trace_count = local_stations * comp_count
    own_index = lax.axis_index("pairs")
    mine = flip_lanes(whitened).reshape(local_stations, comp_count * window_count * window_len)
    asked_of_me = lax.dynamic_index_in_dim(requested, own_index, axis=1, keepdims=False).reshape(-1)
    pick_send = (asked_of_me[:, None] == jnp.arange(local_stations, dtype=jnp.int32)[None, :])
    outgoing = jnp.dot(pick_send.astype(jnp.bfloat16), mine, preferred_element_type=jnp.float32)
    outgoing = outgoing.astype(jnp.bfloat16).reshape(owners, capacity * comp_count, window_count * window_len)
    arrived = lax.all_to_all(outgoing, "pairs", 0, 0, tiled=True)
    trace_pool = arrived.reshape(owners * capacity * comp_count, window_count * window_len)
    row_ids = (partners[0] * comp_count + codes[0]).reshape(-1)
    live_rows = (jnp.arange(per_trace, dtype=jnp.int32)[None, :] < counts[0][:, None]).reshape(-1)
    pool_rows = owners * capacity * comp_count
    pick_recv = (row_ids[:, None] == jnp.arange(pool_rows, dtype=jnp.int32)[None, :]) & live_rows[:, None]
    picked = jnp.dot(pick_recv.astype(jnp.bfloat16), trace_pool, preferred_element_type=jnp.float32)
    picked = picked.astype(jnp.bfloat16).reshape(trace_count, per_trace, window_len)
    half = LAGS // 2
    own = whitened.reshape(trace_count, window_len).astype(jnp.float32)
    span = ((window_len + LAGS + LANE - 1) // LANE) * LANE
    src = jnp.pad(own, ((0, 0), (half, span - window_len - half)))
    total_windows = window_count * tm_count
    scale = 1.0 / math.sqrt(window_len * total_windows)
    lagged = correlate(src, picked, scale)
    block_rows = trace_count * per_trace // tm_count
    lagged = lagged.reshape(chips, cores, block_rows, LAGS)
    core = lax.axis_index("c")
    kept = lax.dynamic_index_in_dim(lagged, core, axis=1, keepdims=False)
    given = lax.dynamic_index_in_dim(lagged, cores - 1 - core, axis=1, keepdims=False)
    got = lax.ppermute(given, "c", [(0, 1), (1, 0)])
    chip_sums = (kept + got).astype(jnp.bfloat16)
    arrived_sums = lax.all_to_all(chip_sums, "z", 0, 0, tiled=True)
    return jnp.sum(arrived_sums.astype(jnp.float32), axis=0, keepdims=True)


def solution(mesh):
    tm_count = mesh.shape["tm"]
    split = jax.sharding.Mesh(
        mesh.devices.reshape(tm_count // 2, 2, mesh.shape["pairs"]), ("z", "c", "pairs")
    )
    tm = ("z", "c")
    return jax.shard_map(
        shards,
        mesh=split,
        in_specs=(
            P("pairs", None, tm, None),
            P(),
            P("pairs", None, None),
            P("pairs", None, None),
            P("pairs", None),
        ),
        out_specs=P("pairs", tm, None),
        check_vma=False,
    )
```

```python
import math

import jax
import jax.numpy as jnp
from jax import lax
from jax.experimental import pallas as pl
from jax.experimental.pallas import tpu as pltpu
from jax.sharding import PartitionSpec as P

LAGS = 1024
BLK = 256
LANE = 128


def normalize(traces):
    values = traces.astype(jnp.float32)
    values = values - jnp.mean(values, axis=-1, keepdims=True)
    power_mean = jnp.mean(values * values, axis=-1, keepdims=True)
    return (values * lax.rsqrt(power_mean + 1e-06)).astype(jnp.bfloat16)


def flip_lanes(rows):
    shape = rows.shape
    grouped = rows.reshape(shape[:-1] + (shape[-1] // LANE, LANE))
    return grouped[..., ::-1].reshape(shape)


def corr_kernel(src_ref, p_ref, o_ref, *, win, scale):
    rows = p_ref.shape[1]
    span = src_ref.shape[2]
    m_blocks = win // BLK
    o_blocks = LAGS // BLK
    d_blocks = m_blocks + o_blocks - 1
    width = BLK * (d_blocks - 1) + BLK + LANE
    wide = jnp.broadcast_to(src_ref[0], (LANE, span))
    hank = pltpu.roll(wide, span - (LANE - 1), 1, stride=1, stride_axis=0)
    hank = hank[:, :width].astype(jnp.bfloat16)
    acc = [jnp.zeros((rows, BLK), jnp.float32) for _ in range(o_blocks)]
    for d in range(d_blocks):
        rhs = jnp.concatenate(
            [hank[:, BLK * d: BLK * d + BLK], hank[:, BLK * d + LANE: BLK * d + LANE + BLK]], axis=0
        )
        lags = [o for o in range(o_blocks) if 0 <= d - o < m_blocks]
        lhs = jnp.concatenate([p_ref[0, :, BLK * (d - o): BLK * (d - o) + BLK] for o in lags], axis=0)
        res = jnp.dot(lhs, rhs, preferred_element_type=jnp.float32)
        for k, o in enumerate(lags):
            acc[o] = acc[o] + res[rows * k: rows * (k + 1)]
    o_ref[0] = jnp.concatenate(acc, axis=1) * scale


def correlate(src, partner_rows, scale):
    traces, rows, win = partner_rows.shape
    span = src.shape[-1]
    flops = 2 * traces * rows * win * LAGS
    return pl.pallas_call(
        lambda s, p, o: corr_kernel(s, p, o, win=win, scale=scale),
        grid=(traces,),
        in_specs=[
            pl.BlockSpec((1, 1, span), lambda j: (j, 0, 0)),
            pl.BlockSpec((1, rows, win), lambda j: (j, 0, 0)),
        ],
        out_specs=pl.BlockSpec((1, rows, LAGS), lambda j: (j, 0, 0)),
        out_shape=jax.ShapeDtypeStruct((traces, rows, LAGS), jnp.float32),
        cost_estimate=pl.CostEstimate(
            flops=flops, transcendentals=0,
            bytes_accessed=traces * (rows * win * 2 + span * 4 + rows * LAGS * 4),
        ),
        name="xcorr",
    )(src.reshape(traces, 1, span), partner_rows)


def shards(record, requested, partners, codes, counts):
    whitened = normalize(record)
    local_stations, comp_count, window_count, window_len = whitened.shape
    owners = lax.axis_size("pairs")
    chips = lax.axis_size("z")
    cores = lax.axis_size("c")
    tm_count = chips * cores
    capacity = requested.shape[2]
    per_trace = partners.shape[2]
    trace_count = local_stations * comp_count
    own_index = lax.axis_index("pairs")
    mine = flip_lanes(whitened).reshape(local_stations, comp_count * window_count * window_len)
    asked_of_me = lax.dynamic_index_in_dim(requested, own_index, axis=1, keepdims=False).reshape(-1)
    pick_send = (asked_of_me[:, None] == jnp.arange(local_stations, dtype=jnp.int32)[None, :])
    outgoing = jnp.dot(pick_send.astype(jnp.bfloat16), mine, preferred_element_type=jnp.float32)
    per_owner = capacity * comp_count * window_count * window_len
    outgoing = outgoing.astype(jnp.bfloat16).reshape(owners, 8, per_owner // 8)
    arrived = lax.all_to_all(outgoing, "pairs", 0, 0, tiled=True)
    trace_pool = arrived.reshape(owners * capacity * comp_count, window_count * window_len)
    row_ids = (partners[0] * comp_count + codes[0]).reshape(-1)
    live_rows = (jnp.arange(per_trace, dtype=jnp.int32)[None, :] < counts[0][:, None]).reshape(-1)
    pool_rows = owners * capacity * comp_count
    pick_recv = (row_ids[:, None] == jnp.arange(pool_rows, dtype=jnp.int32)[None, :]) & live_rows[:, None]
    picked = jnp.dot(pick_recv.astype(jnp.bfloat16), trace_pool, preferred_element_type=jnp.float32)
    picked = picked.astype(jnp.bfloat16).reshape(trace_count, per_trace, window_len)
    half = LAGS // 2
    own = whitened.reshape(trace_count, window_len).astype(jnp.float32)
    span = ((window_len + LAGS + LANE - 1) // LANE) * LANE
    src = jnp.pad(own, ((0, 0), (half, span - window_len - half)))
    total_windows = window_count * tm_count
    scale = 1.0 / math.sqrt(window_len * total_windows)
    lagged = correlate(src, picked, scale)
    block_rows = trace_count * per_trace // tm_count
    lagged = lagged.reshape(chips, cores, block_rows, LAGS)
    core = lax.axis_index("c")
    kept = lax.dynamic_index_in_dim(lagged, core, axis=1, keepdims=False)
    given = lax.dynamic_index_in_dim(lagged, cores - 1 - core, axis=1, keepdims=False)
    got = lax.ppermute(given, "c", [(0, 1), (1, 0)])
    chip_sums = (kept + got).astype(jnp.bfloat16).reshape(chips, 32, block_rows * LAGS // 32)
    arrived_sums = lax.all_to_all(chip_sums, "z", 0, 0, tiled=True)
    total = jnp.sum(arrived_sums.astype(jnp.float32), axis=0)
    return total.reshape(1, block_rows, LAGS)


def solution(mesh):
    tm_count = mesh.shape["tm"]
    split = jax.sharding.Mesh(
        mesh.devices.reshape(tm_count // 2, 2, mesh.shape["pairs"]), ("z", "c", "pairs")
    )
    tm = ("z", "c")
    return jax.shard_map(
        shards,
        mesh=split,
        in_specs=(
            P("pairs", None, tm, None),
            P(),
            P("pairs", None, None),
            P("pairs", None, None),
            P("pairs", None),
        ),
        out_specs=P("pairs", tm, None),
        check_vma=False,
    )
```

```python
import math

import jax
import jax.numpy as jnp
from jax import lax
from jax.experimental import pallas as pl
from jax.experimental.pallas import tpu as pltpu
from jax.sharding import PartitionSpec as P

LAGS = 1024
BLK = 256
LANE = 128


def normalize(traces):
    values = traces.astype(jnp.float32)
    values = values - jnp.mean(values, axis=-1, keepdims=True)
    power_mean = jnp.mean(values * values, axis=-1, keepdims=True)
    return (values * lax.rsqrt(power_mean + 1e-06)).astype(jnp.bfloat16)


def flip_lanes(rows):
    shape = rows.shape
    grouped = rows.reshape(shape[:-1] + (shape[-1] // LANE, LANE))
    return grouped[..., ::-1].reshape(shape)


def trace_corr(src_row, p_ref, u, rows, win):
    span = src_row.shape[1]
    m_blocks = win // BLK
    o_blocks = LAGS // BLK
    d_blocks = m_blocks + o_blocks - 1
    width = BLK * (d_blocks - 1) + BLK + LANE
    wide = jnp.broadcast_to(src_row, (LANE, span))
    hank = pltpu.roll(wide, span - (LANE - 1), 1, stride=1, stride_axis=0)
    hank = hank[:, :width].astype(jnp.bfloat16)
    acc = [jnp.zeros((rows, BLK), jnp.float32) for _ in range(o_blocks)]
    for d in range(d_blocks):
        rhs = jnp.concatenate(
            [hank[:, BLK * d: BLK * d + BLK], hank[:, BLK * d + LANE: BLK * d + LANE + BLK]], axis=0
        )
        lags = [o for o in range(o_blocks) if 0 <= d - o < m_blocks]
        lhs = jnp.concatenate([p_ref[u, :, BLK * (d - o): BLK * (d - o) + BLK] for o in lags], axis=0)
        res = jnp.dot(lhs, rhs, preferred_element_type=jnp.float32)
        for k, o in enumerate(lags):
            acc[o] = acc[o] + res[rows * k: rows * (k + 1)]
    return jnp.concatenate(acc, axis=1)


def corr_kernel(src_ref, p_ref, o_ref, *, win, scale, block_rows):
    group, rows = p_ref.shape[0], p_ref.shape[1]
    pad = o_ref.shape[1] - block_rows
    if pad:
        for blk in range(o_ref.shape[0]):
            o_ref[blk, block_rows:, :] = jnp.zeros((pad, LAGS), jnp.float32)
    for u in range(group):
        cc = trace_corr(src_ref[u], p_ref, u, rows, win) * scale
        first = u * rows
        while first < (u + 1) * rows:
            blk, at = divmod(first, block_rows)
            take = min(block_rows - at, (u + 1) * rows - first)
            o_ref[blk, at: at + take, :] = cc[first - u * rows: first - u * rows + take]
            first += take


def correlate(src, partner_rows, scale, block_rows):
    traces, rows, win = partner_rows.shape
    span = src.shape[-1]
    group = block_rows // math.gcd(block_rows, rows)
    blocks = group * rows // block_rows
    padded = -(-block_rows // 8) * 8
    flops = 2 * traces * rows * win * LAGS
    return pl.pallas_call(
        lambda s, p, o: corr_kernel(s, p, o, win=win, scale=scale, block_rows=block_rows),
        grid=(traces // group,),
        in_specs=[
            pl.BlockSpec((group, 1, span), lambda g: (g, 0, 0)),
            pl.BlockSpec((group, rows, win), lambda g: (g, 0, 0)),
        ],
        out_specs=pl.BlockSpec((blocks, padded, LAGS), lambda g: (g, 0, 0)),
        out_shape=jax.ShapeDtypeStruct((traces * rows // block_rows, padded, LAGS), jnp.float32),
        cost_estimate=pl.CostEstimate(
            flops=flops, transcendentals=0,
            bytes_accessed=traces * (rows * win * 2 + span * 4 + rows * LAGS * 4),
        ),
        name="xcorr",
    )(src.reshape(traces, 1, span), partner_rows)


def shards(record, requested, partners, codes, counts):
    whitened = normalize(record)
    local_stations, comp_count, window_count, window_len = whitened.shape
    owners = lax.axis_size("pairs")
    chips = lax.axis_size("z")
    cores = lax.axis_size("c")
    tm_count = chips * cores
    capacity = requested.shape[2]
    per_trace = partners.shape[2]
    trace_count = local_stations * comp_count
    own_index = lax.axis_index("pairs")
    per_station = comp_count * window_count * window_len
    mine = flip_lanes(whitened).reshape(local_stations, 8, per_station // 8)
    asked_of_me = lax.dynamic_index_in_dim(requested, own_index, axis=1, keepdims=False)
    pick_send = (asked_of_me[:, :, None] == jnp.arange(local_stations, dtype=jnp.int32)[None, None, :])
    outgoing = jnp.einsum("eis,sru->eiru", pick_send.astype(jnp.bfloat16), mine,
                          preferred_element_type=jnp.float32)
    outgoing = outgoing.astype(jnp.bfloat16).reshape(owners, capacity * 8, per_station // 8)
    arrived = lax.all_to_all(outgoing, "pairs", 0, 0, tiled=True)
    trace_pool = arrived.reshape(owners * capacity * comp_count, window_count * window_len)
    row_ids = (partners[0] * comp_count + codes[0]).reshape(-1)
    live_rows = (jnp.arange(per_trace, dtype=jnp.int32)[None, :] < counts[0][:, None]).reshape(-1)
    pool_rows = owners * capacity * comp_count
    pick_recv = (row_ids[:, None] == jnp.arange(pool_rows, dtype=jnp.int32)[None, :]) & live_rows[:, None]
    picked = jnp.dot(pick_recv.astype(jnp.bfloat16), trace_pool, preferred_element_type=jnp.float32)
    picked = picked.astype(jnp.bfloat16).reshape(trace_count, per_trace, window_len)
    half = LAGS // 2
    own = whitened.reshape(trace_count, window_len).astype(jnp.float32)
    span = ((window_len + LAGS + LANE - 1) // LANE) * LANE
    src = jnp.pad(own, ((0, 0), (half, span - window_len - half)))
    total_windows = window_count * tm_count
    scale = 1.0 / math.sqrt(window_len * total_windows)
    block_rows = trace_count * per_trace // tm_count
    lagged = correlate(src, picked, scale, block_rows)
    lagged = lagged.reshape(chips, cores, lagged.shape[1], LAGS)
    core = lax.axis_index("c")
    kept = lax.dynamic_index_in_dim(lagged, core, axis=1, keepdims=False)
    given = lax.dynamic_index_in_dim(lagged, cores - 1 - core, axis=1, keepdims=False)
    got = lax.ppermute(given, "c", [(0, 1), (1, 0)])
    chip_sums = (kept + got)[:, :block_rows].astype(jnp.bfloat16).reshape(chips, 32, block_rows * LAGS // 32)
    arrived_sums = lax.all_to_all(chip_sums, "z", 0, 0, tiled=True)
    total = jnp.sum(arrived_sums.astype(jnp.float32), axis=0)
    return total.reshape(1, block_rows, LAGS)


def solution(mesh):
    tm_count = mesh.shape["tm"]
    split = jax.sharding.Mesh(
        mesh.devices.reshape(tm_count // 2, 2, mesh.shape["pairs"]), ("z", "c", "pairs")
    )
    tm = ("z", "c")
    return jax.shard_map(
        shards,
        mesh=split,
        in_specs=(
            P("pairs", None, tm, None),
            P(),
            P("pairs", None, None),
            P("pairs", None, None),
            P("pairs", None),
        ),
        out_specs=P("pairs", tm, None),
        check_vma=False,
    )
```

```python
import math

import jax
import jax.numpy as jnp
from jax import lax
from jax.experimental import pallas as pl
from jax.experimental.pallas import tpu as pltpu
from jax.sharding import PartitionSpec as P

LAGS = 1024
BLK = 256
LANE = 128


def normalize(traces):
    values = traces.astype(jnp.float32)
    values = values - jnp.mean(values, axis=-1, keepdims=True)
    power_mean = jnp.mean(values * values, axis=-1, keepdims=True)
    return (values * lax.rsqrt(power_mean + 1e-06)).astype(jnp.bfloat16)


def flip_lanes(rows):
    shape = rows.shape
    grouped = rows.reshape(shape[:-1] + (shape[-1] // LANE, LANE))
    return grouped[..., ::-1].reshape(shape)


def trace_corr(src_row, p_ref, u, rows, win):
    span = src_row.shape[1]
    m_blocks = win // BLK
    o_blocks = LAGS // BLK
    d_blocks = m_blocks + o_blocks - 1
    width = BLK * (d_blocks - 1) + BLK + LANE
    wide = jnp.broadcast_to(src_row, (LANE, span))
    hank = pltpu.roll(wide, span - (LANE - 1), 1, stride=1, stride_axis=0)
    hank = hank[:, :width].astype(jnp.bfloat16)
    acc = [jnp.zeros((rows, BLK), jnp.float32) for _ in range(o_blocks)]
    for d in range(d_blocks):
        rhs = jnp.concatenate(
            [hank[:, BLK * d: BLK * d + BLK], hank[:, BLK * d + LANE: BLK * d + LANE + BLK]], axis=0
        )
        lags = [o for o in range(o_blocks) if 0 <= d - o < m_blocks]
        lhs = jnp.concatenate([p_ref[u, :, BLK * (d - o): BLK * (d - o) + BLK] for o in lags], axis=0)
        res = jnp.dot(lhs, rhs, preferred_element_type=jnp.float32)
        for k, o in enumerate(lags):
            acc[o] = acc[o] + res[rows * k: rows * (k + 1)]
    return jnp.concatenate(acc, axis=1)


def corr_kernel(src_ref, p_ref, o_ref, *, win, scale, block_rows):
    group, rows = p_ref.shape[0], p_ref.shape[1]
    pad = o_ref.shape[1] - block_rows
    if pad:
        for blk in range(o_ref.shape[0]):
            o_ref[blk, block_rows:, :] = jnp.zeros((pad, LAGS), jnp.float32)
    for u in range(group):
        cc = trace_corr(src_ref[u], p_ref, u, rows, win) * scale
        first = u * rows
        while first < (u + 1) * rows:
            blk, at = divmod(first, block_rows)
            take = min(block_rows - at, (u + 1) * rows - first)
            o_ref[blk, at: at + take, :] = cc[first - u * rows: first - u * rows + take]
            first += take


def correlate(src, partner_rows, scale, block_rows):
    traces, rows, win = partner_rows.shape
    span = src.shape[-1]
    group = 2 * block_rows // math.gcd(block_rows, rows)
    blocks = group * rows // block_rows
    padded = -(-block_rows // 8) * 8
    flops = 2 * traces * rows * win * LAGS
    return pl.pallas_call(
        lambda s, p, o: corr_kernel(s, p, o, win=win, scale=scale, block_rows=block_rows),
        grid=(traces // group,),
        in_specs=[
            pl.BlockSpec((group, 1, span), lambda g: (g, 0, 0)),
            pl.BlockSpec((group, rows, win), lambda g: (g, 0, 0)),
        ],
        out_specs=pl.BlockSpec((blocks, padded, LAGS), lambda g: (g, 0, 0)),
        out_shape=jax.ShapeDtypeStruct((traces * rows // block_rows, padded, LAGS), jnp.float32),
        cost_estimate=pl.CostEstimate(
            flops=flops, transcendentals=0,
            bytes_accessed=traces * (rows * win * 2 + span * 4 + rows * LAGS * 4),
        ),
        name="xcorr",
    )(src.reshape(traces, 1, span), partner_rows)


def shards(record, requested, partners, codes, counts):
    whitened = normalize(record)
    local_stations, comp_count, window_count, window_len = whitened.shape
    owners = lax.axis_size("pairs")
    chips = lax.axis_size("z")
    cores = lax.axis_size("c")
    tm_count = chips * cores
    capacity = requested.shape[2]
    per_trace = partners.shape[2]
    trace_count = local_stations * comp_count
    own_index = lax.axis_index("pairs")
    per_station = comp_count * window_count * window_len
    mine = flip_lanes(whitened).reshape(local_stations, 8, per_station // 8)
    asked_of_me = lax.dynamic_index_in_dim(requested, own_index, axis=1, keepdims=False)
    outgoing = jnp.broadcast_to(mine[0], (owners, capacity) + mine.shape[1:])
    for station in range(1, local_stations):
        outgoing = jnp.where((asked_of_me == station)[:, :, None, None], mine[station], outgoing)
    outgoing = outgoing.reshape(owners, capacity * 8, per_station // 8)
    arrived = lax.all_to_all(outgoing, "pairs", 0, 0, tiled=True)
    trace_pool = arrived.reshape(owners * capacity * comp_count, window_count * window_len)
    row_ids = (partners[0] * comp_count + codes[0]).reshape(-1)
    live_rows = (jnp.arange(per_trace, dtype=jnp.int32)[None, :] < counts[0][:, None]).reshape(-1)
    pool_rows = owners * capacity * comp_count
    pick_recv = (row_ids[:, None] == jnp.arange(pool_rows, dtype=jnp.int32)[None, :]) & live_rows[:, None]
    picked = jnp.dot(pick_recv.astype(jnp.bfloat16), trace_pool, preferred_element_type=jnp.float32)
    picked = picked.astype(jnp.bfloat16).reshape(trace_count, per_trace, window_len)
    half = LAGS // 2
    own = whitened.reshape(trace_count, window_len).astype(jnp.float32)
    span = ((window_len + LAGS + LANE - 1) // LANE) * LANE
    src = jnp.pad(own, ((0, 0), (half, span - window_len - half)))
    total_windows = window_count * tm_count
    scale = 1.0 / math.sqrt(window_len * total_windows)
    block_rows = trace_count * per_trace // tm_count
    lagged = correlate(src, picked, scale, block_rows)
    lagged = lagged.reshape(chips, cores, lagged.shape[1], LAGS)
    core = lax.axis_index("c")
    kept = lax.dynamic_index_in_dim(lagged, core, axis=1, keepdims=False)
    given = lax.dynamic_index_in_dim(lagged, cores - 1 - core, axis=1, keepdims=False)
    got = lax.ppermute(given, "c", [(0, 1), (1, 0)])
    chip_sums = (kept + got)[:, :block_rows].astype(jnp.bfloat16).reshape(chips, 32, block_rows * LAGS // 32)
    arrived_sums = lax.all_to_all(chip_sums, "z", 0, 0, tiled=True)
    total = jnp.sum(arrived_sums.astype(jnp.float32), axis=0)
    return total.reshape(1, block_rows, LAGS)


def solution(mesh):
    tm_count = mesh.shape["tm"]
    split = jax.sharding.Mesh(
        mesh.devices.reshape(tm_count // 2, 2, mesh.shape["pairs"]), ("z", "c", "pairs")
    )
    tm = ("z", "c")
    return jax.shard_map(
        shards,
        mesh=split,
        in_specs=(
            P("pairs", None, tm, None),
            P(),
            P("pairs", None, None),
            P("pairs", None, None),
            P("pairs", None),
        ),
        out_specs=P("pairs", tm, None),
        check_vma=False,
    )
```

```python
import math

import jax
import jax.numpy as jnp
from jax import lax
from jax.experimental import pallas as pl
from jax.experimental.pallas import tpu as pltpu
from jax.sharding import PartitionSpec as P

LAGS = 1024
BLK = 256
LANE = 128


def normalize(traces):
    values = traces.astype(jnp.float32)
    values = values - jnp.mean(values, axis=-1, keepdims=True)
    power_mean = jnp.mean(values * values, axis=-1, keepdims=True)
    return (values * lax.rsqrt(power_mean + 1e-06)).astype(jnp.bfloat16)


def flip_lanes(rows):
    shape = rows.shape
    grouped = rows.reshape(shape[:-1] + (shape[-1] // LANE, LANE))
    return grouped[..., ::-1].reshape(shape)


def trace_corr(src_row, p_ref, u, rows, win):
    span = src_row.shape[1]
    m_blocks = win // BLK
    o_blocks = LAGS // BLK
    d_blocks = m_blocks + o_blocks - 1
    width = BLK * (d_blocks - 1) + BLK + LANE
    wide = jnp.broadcast_to(src_row, (LANE, span))
    hank = pltpu.roll(wide, span - (LANE - 1), 1, stride=1, stride_axis=0)
    hank = hank[:, :width].astype(jnp.bfloat16)
    acc = [jnp.zeros((rows, BLK), jnp.float32) for _ in range(o_blocks)]
    for d in range(d_blocks):
        rhs = jnp.concatenate(
            [hank[:, BLK * d: BLK * d + BLK], hank[:, BLK * d + LANE: BLK * d + LANE + BLK]], axis=0
        )
        lags = [o for o in range(o_blocks) if 0 <= d - o < m_blocks]
        lhs = jnp.concatenate([p_ref[u, :, BLK * (d - o): BLK * (d - o) + BLK] for o in lags], axis=0)
        res = jnp.dot(lhs, rhs, preferred_element_type=jnp.float32)
        for k, o in enumerate(lags):
            acc[o] = acc[o] + res[rows * k: rows * (k + 1)]
    return jnp.concatenate(acc, axis=1)


def corr_kernel(core_ref, src_ref, p_ref, kept_ref, sent_ref, *, win, scale, block_rows):
    group, rows = p_ref.shape[0], p_ref.shape[1]
    core = core_ref[0]
    pad = kept_ref.shape[1] - block_rows
    if pad:
        for half in range(kept_ref.shape[0]):
            kept_ref[half, block_rows:, :] = jnp.zeros((pad, LAGS), jnp.float32)
            sent_ref[half, block_rows:, :] = jnp.zeros((pad, LAGS), jnp.float32)
    for u in range(group):
        cc = trace_corr(src_ref[u], p_ref, u, rows, win) * scale
        first = u * rows
        while first < (u + 1) * rows:
            blk, at = divmod(first, block_rows)
            take = min(block_rows - at, (u + 1) * rows - first)
            piece = cc[first - u * rows: first - u * rows + take]
            parity = blk % 2

            @pl.when(core == parity)
            def _():
                kept_ref[blk // 2, at: at + take, :] = piece

            @pl.when(core != parity)
            def _():
                sent_ref[blk // 2, at: at + take, :] = piece

            first += take


def correlate(core, src, partner_rows, scale, block_rows):
    traces, rows, win = partner_rows.shape
    span = src.shape[-1]
    group = block_rows // math.gcd(block_rows, rows)
    blocks = group * rows // block_rows
    if blocks % 2:
        group, blocks = 2 * group, 2 * blocks
    padded = -(-block_rows // 8) * 8
    flops = 2 * traces * rows * win * LAGS
    half_shape = jax.ShapeDtypeStruct((traces * rows // block_rows // 2, padded, LAGS), jnp.float32)
    out_spec = pl.BlockSpec((blocks // 2, padded, LAGS), lambda g, c: (g, 0, 0))
    return pl.pallas_call(
        lambda c, s, p, k, o: corr_kernel(c, s, p, k, o, win=win, scale=scale, block_rows=block_rows),
        grid_spec=pltpu.PrefetchScalarGridSpec(
            num_scalar_prefetch=1,
            grid=(traces // group,),
            in_specs=[
                pl.BlockSpec((group, 1, span), lambda g, c: (g, 0, 0)),
                pl.BlockSpec((group, rows, win), lambda g, c: (g, 0, 0)),
            ],
            out_specs=[out_spec, out_spec],
        ),
        out_shape=[half_shape, half_shape],
        cost_estimate=pl.CostEstimate(
            flops=flops, transcendentals=0,
            bytes_accessed=traces * (rows * win * 2 + span * 4 + rows * LAGS * 4),
        ),
        name="xcorr",
    )(core.reshape(1), src.reshape(traces, 1, span), partner_rows)


def pick_kernel(ids_ref, rows_ref, o_ref):
    def body(k, carry):
        o_ref[k] = rows_ref[ids_ref[k]]
        return carry

    lax.fori_loop(0, o_ref.shape[0], body, 0)


def pick_rows(ids, rows):
    count = ids.shape[0]
    slab = rows.shape[1:]
    zeros = (0,) * len(slab)
    return pl.pallas_call(
        pick_kernel,
        grid_spec=pltpu.PrefetchScalarGridSpec(
            num_scalar_prefetch=1,
            grid=(1,),
            in_specs=[pl.BlockSpec(rows.shape, lambda i, ids: (0,) + zeros)],
            out_specs=pl.BlockSpec((count,) + slab, lambda i, ids: (0,) + zeros),
        ),
        out_shape=jax.ShapeDtypeStruct((count,) + slab, rows.dtype),
        name="pick_rows",
    )(ids, rows)


def shards(record, requested, partners, codes, counts):
    whitened = normalize(record)
    local_stations, comp_count, window_count, window_len = whitened.shape
    owners = lax.axis_size("pairs")
    chips = lax.axis_size("z")
    cores = lax.axis_size("c")
    tm_count = chips * cores
    capacity = requested.shape[2]
    per_trace = partners.shape[2]
    trace_count = local_stations * comp_count
    own_index = lax.axis_index("pairs")
    per_station = comp_count * window_count * window_len
    mine = flip_lanes(whitened).reshape(local_stations, 8, per_station // 8)
    asked_of_me = lax.dynamic_index_in_dim(requested, own_index, axis=1, keepdims=False)
    outgoing = pick_rows(asked_of_me.reshape(-1), mine)
    arrived = lax.all_to_all(outgoing, "pairs", 0, 0, tiled=True)
    trace_pool = arrived.reshape(owners * capacity * comp_count, window_count * window_len)
    row_ids = (partners[0] * comp_count + codes[0]).reshape(-1)
    live_rows = (jnp.arange(per_trace, dtype=jnp.int32)[None, :] < counts[0][:, None]).reshape(-1)
    pool_rows = owners * capacity * comp_count
    pick_recv = (row_ids[:, None] == jnp.arange(pool_rows, dtype=jnp.int32)[None, :]) & live_rows[:, None]
    picked = jnp.dot(pick_recv.astype(jnp.bfloat16), trace_pool, preferred_element_type=jnp.float32)
    picked = picked.astype(jnp.bfloat16).reshape(trace_count, per_trace, window_len)
    half = LAGS // 2
    own = whitened.reshape(trace_count, window_len).astype(jnp.float32)
    span = ((window_len + LAGS + LANE - 1) // LANE) * LANE
    src = jnp.pad(own, ((0, 0), (half, span - window_len - half)))
    total_windows = window_count * tm_count
    scale = 1.0 / math.sqrt(window_len * total_windows)
    block_rows = trace_count * per_trace // tm_count
    core = lax.axis_index("c").astype(jnp.int32)
    kept, given = correlate(core, src, picked, scale, block_rows)
    got = lax.ppermute(given, "c", [(0, 1), (1, 0)])
    chip_sums = (kept + got)[:, :block_rows].astype(jnp.bfloat16).reshape(chips, 32, block_rows * LAGS // 32)
    arrived_sums = lax.all_to_all(chip_sums, "z", 0, 0, tiled=True)
    total = jnp.sum(arrived_sums.astype(jnp.float32), axis=0)
    return total.reshape(1, block_rows, LAGS)


def solution(mesh):
    tm_count = mesh.shape["tm"]
    split = jax.sharding.Mesh(
        mesh.devices.reshape(tm_count // 2, 2, mesh.shape["pairs"]), ("z", "c", "pairs")
    )
    tm = ("z", "c")
    return jax.shard_map(
        shards,
        mesh=split,
        in_specs=(
            P("pairs", None, tm, None),
            P(),
            P("pairs", None, None),
            P("pairs", None, None),
            P("pairs", None),
        ),
        out_specs=P("pairs", tm, None),
        check_vma=False,
    )
```

```python
import math

import jax
import jax.numpy as jnp
from jax import lax
from jax.experimental import pallas as pl
from jax.experimental.pallas import tpu as pltpu
from jax.sharding import PartitionSpec as P

LAGS = 1024
BLK = 256
LANE = 128


def normalize(traces):
    values = traces.astype(jnp.float32)
    values = values - jnp.mean(values, axis=-1, keepdims=True)
    power_mean = jnp.mean(values * values, axis=-1, keepdims=True)
    return (values * lax.rsqrt(power_mean + 1e-06)).astype(jnp.bfloat16)


def flip_lanes(rows):
    shape = rows.shape
    grouped = rows.reshape(shape[:-1] + (shape[-1] // LANE, LANE))
    return grouped[..., ::-1].reshape(shape)


def trace_corr(src_row, p_ref, u, rows, win):
    span = src_row.shape[1]
    m_blocks = win // BLK
    o_blocks = LAGS // BLK
    d_blocks = m_blocks + o_blocks - 1
    width = BLK * (d_blocks - 1) + BLK + LANE
    wide = jnp.broadcast_to(src_row, (LANE, span))
    hank = pltpu.roll(wide, span - (LANE - 1), 1, stride=1, stride_axis=0)
    hank = hank[:, :width].astype(jnp.bfloat16)
    acc = [jnp.zeros((rows, BLK), jnp.float32) for _ in range(o_blocks)]
    for d in range(d_blocks):
        rhs = jnp.concatenate(
            [hank[:, BLK * d: BLK * d + BLK], hank[:, BLK * d + LANE: BLK * d + LANE + BLK]], axis=0
        )
        lags = [o for o in range(o_blocks) if 0 <= d - o < m_blocks]
        lhs = jnp.concatenate([p_ref[u, :, BLK * (d - o): BLK * (d - o) + BLK] for o in lags], axis=0)
        res = jnp.dot(lhs, rhs, preferred_element_type=jnp.float32)
        for k, o in enumerate(lags):
            acc[o] = acc[o] + res[rows * k: rows * (k + 1)]
    return jnp.concatenate(acc, axis=1)


def corr_kernel(src_ref, p_ref, o_ref, *, win, scale, block_rows):
    group, rows = p_ref.shape[0], p_ref.shape[1]
    pad = o_ref.shape[2] - block_rows
    if pad:
        for parity in range(2):
            for blk in range(o_ref.shape[1]):
                o_ref[parity, blk, block_rows:, :] = jnp.zeros((pad, LAGS), jnp.float32)
    for u in range(group):
        cc = trace_corr(src_ref[u], p_ref, u, rows, win) * scale
        first = u * rows
        while first < (u + 1) * rows:
            blk, at = divmod(first, block_rows)
            take = min(block_rows - at, (u + 1) * rows - first)
            o_ref[blk % 2, blk // 2, at: at + take, :] = cc[first - u * rows: first - u * rows + take]
            first += take


def correlate(src, partner_rows, scale, block_rows):
    traces, rows, win = partner_rows.shape
    span = src.shape[-1]
    group = block_rows // math.gcd(block_rows, rows)
    blocks = group * rows // block_rows
    if blocks % 2:
        group, blocks = 2 * group, 2 * blocks
    padded = -(-block_rows // 8) * 8
    flops = 2 * traces * rows * win * LAGS
    return pl.pallas_call(
        lambda s, p, o: corr_kernel(s, p, o, win=win, scale=scale, block_rows=block_rows),
        grid=(traces // group,),
        in_specs=[
            pl.BlockSpec((group, 1, span), lambda g: (g, 0, 0)),
            pl.BlockSpec((group, rows, win), lambda g: (g, 0, 0)),
        ],
        out_specs=pl.BlockSpec((2, blocks // 2, padded, LAGS), lambda g: (0, g, 0, 0)),
        out_shape=jax.ShapeDtypeStruct((2, traces * rows // block_rows // 2, padded, LAGS), jnp.float32),
        cost_estimate=pl.CostEstimate(
            flops=flops, transcendentals=0,
            bytes_accessed=traces * (rows * win * 2 + span * 4 + rows * LAGS * 4),
        ),
        name="xcorr",
    )(src.reshape(traces, 1, span), partner_rows)


def shards(record, requested, partners, codes, counts):
    whitened = normalize(record)
    local_stations, comp_count, window_count, window_len = whitened.shape
    owners = lax.axis_size("pairs")
    chips = lax.axis_size("z")
    cores = lax.axis_size("c")
    tm_count = chips * cores
    capacity = requested.shape[2]
    per_trace = partners.shape[2]
    trace_count = local_stations * comp_count
    own_index = lax.axis_index("pairs")
    per_station = comp_count * window_count * window_len
    mine = flip_lanes(whitened).reshape(local_stations, 8, per_station // 8)
    asked_of_me = lax.dynamic_index_in_dim(requested, own_index, axis=1, keepdims=False)
    pick_send = (asked_of_me[:, :, None] == jnp.arange(local_stations, dtype=jnp.int32)[None, None, :])
    outgoing = jnp.einsum("eis,sru->eiru", pick_send.astype(jnp.bfloat16), mine,
                          preferred_element_type=jnp.float32)
    outgoing = outgoing.astype(jnp.bfloat16).reshape(owners, capacity * 8, per_station // 8)
    arrived = lax.all_to_all(outgoing, "pairs", 0, 0, tiled=True)
    trace_pool = arrived.reshape(owners * capacity * comp_count, window_count * window_len)
    row_ids = (partners[0] * comp_count + codes[0]).reshape(-1)
    live_rows = (jnp.arange(per_trace, dtype=jnp.int32)[None, :] < counts[0][:, None]).reshape(-1)
    pool_rows = owners * capacity * comp_count
    pick_recv = (row_ids[:, None] == jnp.arange(pool_rows, dtype=jnp.int32)[None, :]) & live_rows[:, None]
    picked = jnp.dot(pick_recv.astype(jnp.bfloat16), trace_pool, preferred_element_type=jnp.float32)
    picked = picked.astype(jnp.bfloat16).reshape(trace_count, per_trace, window_len)
    half = LAGS // 2
    own = whitened.reshape(trace_count, window_len).astype(jnp.float32)
    span = ((window_len + LAGS + LANE - 1) // LANE) * LANE
    src = jnp.pad(own, ((0, 0), (half, span - window_len - half)))
    total_windows = window_count * tm_count
    scale = 1.0 / math.sqrt(window_len * total_windows)
    block_rows = trace_count * per_trace // tm_count
    lagged = correlate(src, picked, scale, block_rows)
    core = lax.axis_index("c")
    to_odd = lax.ppermute(lagged[1], "c", [(0, 1)])
    to_even = lax.ppermute(lagged[0], "c", [(1, 0)])
    chip_sums = jnp.where(core == 0, lagged[0] + to_even, lagged[1] + to_odd)
    chip_sums = chip_sums[:, :block_rows].astype(jnp.bfloat16).reshape(chips, 32, block_rows * LAGS // 32)
    arrived_sums = lax.all_to_all(chip_sums, "z", 0, 0, tiled=True)
    total = jnp.sum(arrived_sums.astype(jnp.float32), axis=0)
    return total.reshape(1, block_rows, LAGS)


def solution(mesh):
    tm_count = mesh.shape["tm"]
    split = jax.sharding.Mesh(
        mesh.devices.reshape(tm_count // 2, 2, mesh.shape["pairs"]), ("z", "c", "pairs")
    )
    tm = ("z", "c")
    return jax.shard_map(
        shards,
        mesh=split,
        in_specs=(
            P("pairs", None, tm, None),
            P(),
            P("pairs", None, None),
            P("pairs", None, None),
            P("pairs", None),
        ),
        out_specs=P("pairs", tm, None),
        check_vma=False,
    )
```

```python
import math

import jax
import jax.numpy as jnp
from jax import lax
from jax.experimental import pallas as pl
from jax.experimental.pallas import tpu as pltpu
from jax.sharding import PartitionSpec as P

LAGS = 1024
BLK = 256
LANE = 128


def white_kernel(x_ref, o_ref):
    values = x_ref[...].astype(jnp.float32)
    values = values - jnp.mean(values, axis=-1, keepdims=True)
    power_mean = jnp.mean(values * values, axis=-1, keepdims=True)
    o_ref[...] = (values * lax.rsqrt(power_mean + 1e-06)).astype(o_ref.dtype)


def normalize(traces):
    shape = traces.shape
    rows = traces.reshape(-1, shape[-1])
    out = pl.pallas_call(
        white_kernel,
        out_shape=jax.ShapeDtypeStruct(rows.shape, jnp.bfloat16),
        name="whiten",
    )(rows)
    return out.reshape(shape)


def flip_lanes(rows):
    shape = rows.shape
    grouped = rows.reshape(shape[:-1] + (shape[-1] // LANE, LANE))
    return grouped[..., ::-1].reshape(shape)


def trace_corr(src_row, p_ref, u, rows, win):
    span = src_row.shape[1]
    m_blocks = win // BLK
    o_blocks = LAGS // BLK
    d_blocks = m_blocks + o_blocks - 1
    width = BLK * (d_blocks - 1) + BLK + LANE
    wide = jnp.broadcast_to(src_row, (LANE, span))
    hank = pltpu.roll(wide, span - (LANE - 1), 1, stride=1, stride_axis=0)
    hank = hank[:, :width].astype(jnp.bfloat16)
    acc = [jnp.zeros((rows, BLK), jnp.float32) for _ in range(o_blocks)]
    for d in range(d_blocks):
        rhs = jnp.concatenate(
            [hank[:, BLK * d: BLK * d + BLK], hank[:, BLK * d + LANE: BLK * d + LANE + BLK]], axis=0
        )
        lags = [o for o in range(o_blocks) if 0 <= d - o < m_blocks]
        lhs = jnp.concatenate([p_ref[u, :, BLK * (d - o): BLK * (d - o) + BLK] for o in lags], axis=0)
        res = jnp.dot(lhs, rhs, preferred_element_type=jnp.float32)
        for k, o in enumerate(lags):
            acc[o] = acc[o] + res[rows * k: rows * (k + 1)]
    return jnp.concatenate(acc, axis=1)


def corr_kernel(src_ref, p_ref, o_ref, *, win, scale, block_rows):
    group, rows = p_ref.shape[0], p_ref.shape[1]
    pad = o_ref.shape[1] - block_rows
    if pad:
        for blk in range(o_ref.shape[0]):
            o_ref[blk, block_rows:, :] = jnp.zeros((pad, LAGS), jnp.float32)
    for u in range(group):
        cc = trace_corr(src_ref[u], p_ref, u, rows, win) * scale
        first = u * rows
        while first < (u + 1) * rows:
            blk, at = divmod(first, block_rows)
            take = min(block_rows - at, (u + 1) * rows - first)
            o_ref[blk, at: at + take, :] = cc[first - u * rows: first - u * rows + take]
            first += take


def correlate(src, partner_rows, scale, block_rows):
    traces, rows, win = partner_rows.shape
    span = src.shape[-1]
    group = block_rows // math.gcd(block_rows, rows)
    blocks = group * rows // block_rows
    padded = -(-block_rows // 8) * 8
    flops = 2 * traces * rows * win * LAGS
    return pl.pallas_call(
        lambda s, p, o: corr_kernel(s, p, o, win=win, scale=scale, block_rows=block_rows),
        grid=(traces // group,),
        in_specs=[
            pl.BlockSpec((group, 1, span), lambda g: (g, 0, 0)),
            pl.BlockSpec((group, rows, win), lambda g: (g, 0, 0)),
        ],
        out_specs=pl.BlockSpec((blocks, padded, LAGS), lambda g: (g, 0, 0)),
        out_shape=jax.ShapeDtypeStruct((traces * rows // block_rows, padded, LAGS), jnp.float32),
        cost_estimate=pl.CostEstimate(
            flops=flops, transcendentals=0,
            bytes_accessed=traces * (rows * win * 2 + span * 4 + rows * LAGS * 4),
        ),
        name="xcorr",
    )(src.reshape(traces, 1, span), partner_rows)


def shards(record, requested, partners, codes, counts):
    whitened = normalize(record)
    local_stations, comp_count, window_count, window_len = whitened.shape
    owners = lax.axis_size("pairs")
    chips = lax.axis_size("z")
    cores = lax.axis_size("c")
    tm_count = chips * cores
    capacity = requested.shape[2]
    per_trace = partners.shape[2]
    trace_count = local_stations * comp_count
    own_index = lax.axis_index("pairs")
    per_station = comp_count * window_count * window_len
    mine = flip_lanes(whitened).reshape(local_stations, 8, per_station // 8)
    asked_of_me = lax.dynamic_index_in_dim(requested, own_index, axis=1, keepdims=False)
    pick_send = (asked_of_me[:, :, None] == jnp.arange(local_stations, dtype=jnp.int32)[None, None, :])
    outgoing = jnp.einsum("eis,sru->eiru", pick_send.astype(jnp.bfloat16), mine,
                          preferred_element_type=jnp.float32)
    outgoing = outgoing.astype(jnp.bfloat16).reshape(owners, capacity * 8, per_station // 8)
    arrived = lax.all_to_all(outgoing, "pairs", 0, 0, tiled=True)
    trace_pool = arrived.reshape(owners * capacity * comp_count, window_count * window_len)
    row_ids = (partners[0] * comp_count + codes[0]).reshape(-1)
    live_rows = (jnp.arange(per_trace, dtype=jnp.int32)[None, :] < counts[0][:, None]).reshape(-1)
    pool_rows = owners * capacity * comp_count
    pick_recv = (row_ids[:, None] == jnp.arange(pool_rows, dtype=jnp.int32)[None, :]) & live_rows[:, None]
    picked = jnp.dot(pick_recv.astype(jnp.bfloat16), trace_pool, preferred_element_type=jnp.float32)
    picked = picked.astype(jnp.bfloat16).reshape(trace_count, per_trace, window_len)
    half = LAGS // 2
    own = whitened.reshape(trace_count, window_len).astype(jnp.float32)
    span = ((window_len + LAGS + LANE - 1) // LANE) * LANE
    src = jnp.pad(own, ((0, 0), (half, span - window_len - half)))
    total_windows = window_count * tm_count
    scale = 1.0 / math.sqrt(window_len * total_windows)
    block_rows = trace_count * per_trace // tm_count
    lagged = correlate(src, picked, scale, block_rows)
    lagged = lagged.reshape(chips, cores, lagged.shape[1], LAGS)
    core = lax.axis_index("c")
    kept = lax.dynamic_index_in_dim(lagged, core, axis=1, keepdims=False)
    given = lax.dynamic_index_in_dim(lagged, cores - 1 - core, axis=1, keepdims=False)
    got = lax.ppermute(given, "c", [(0, 1), (1, 0)])
    chip_sums = (kept + got)[:, :block_rows].astype(jnp.bfloat16).reshape(chips, 32, block_rows * LAGS // 32)
    arrived_sums = lax.all_to_all(chip_sums, "z", 0, 0, tiled=True)
    total = jnp.sum(arrived_sums.astype(jnp.float32), axis=0)
    return total.reshape(1, block_rows, LAGS)


def solution(mesh):
    tm_count = mesh.shape["tm"]
    split = jax.sharding.Mesh(
        mesh.devices.reshape(tm_count // 2, 2, mesh.shape["pairs"]), ("z", "c", "pairs")
    )
    tm = ("z", "c")
    return jax.shard_map(
        shards,
        mesh=split,
        in_specs=(
            P("pairs", None, tm, None),
            P(),
            P("pairs", None, None),
            P("pairs", None, None),
            P("pairs", None),
        ),
        out_specs=P("pairs", tm, None),
        check_vma=False,
    )
```

```python
import math

import jax
import jax.numpy as jnp
from jax import lax
from jax.experimental import pallas as pl
from jax.experimental.pallas import tpu as pltpu
from jax.sharding import PartitionSpec as P

LAGS = 1024
BLK = 256
LANE = 128


def normalize(traces):
    values = traces.astype(jnp.float32)
    values = values - jnp.mean(values, axis=-1, keepdims=True)
    power_mean = jnp.mean(values * values, axis=-1, keepdims=True)
    return (values * lax.rsqrt(power_mean + 1e-06)).astype(jnp.bfloat16)


def flip_lanes(rows):
    shape = rows.shape
    grouped = rows.reshape(shape[:-1] + (shape[-1] // LANE, LANE))
    return grouped[..., ::-1].reshape(shape)


def trace_corr(src_row, p_ref, u, rows, win):
    span = src_row.shape[1]
    m_blocks = win // BLK
    o_blocks = LAGS // BLK
    d_blocks = m_blocks + o_blocks - 1
    width = BLK * (d_blocks - 1) + BLK + LANE
    wide = jnp.broadcast_to(src_row, (LANE, span))
    hank = pltpu.roll(wide, span - (LANE - 1), 1, stride=1, stride_axis=0)
    hank = hank[:, :width].astype(jnp.bfloat16)
    acc = [jnp.zeros((rows, BLK), jnp.float32) for _ in range(o_blocks)]
    for d in range(d_blocks):
        rhs = jnp.concatenate(
            [hank[:, BLK * d: BLK * d + BLK], hank[:, BLK * d + LANE: BLK * d + LANE + BLK]], axis=0
        )
        lags = [o for o in range(o_blocks) if 0 <= d - o < m_blocks]
        lhs = jnp.concatenate([p_ref[u, :, BLK * (d - o): BLK * (d - o) + BLK] for o in lags], axis=0)
        res = jnp.dot(lhs, rhs, preferred_element_type=jnp.float32)
        for k, o in enumerate(lags):
            acc[o] = acc[o] + res[rows * k: rows * (k + 1)]
    return jnp.concatenate(acc, axis=1)


def corr_kernel(core_ref, src_ref, p_ref, kept_ref, sent_ref, o_ref, *, win, scale, block_rows):
    group, rows = p_ref.shape[0], p_ref.shape[1]
    pad = o_ref.shape[1] - block_rows
    if pad:
        for blk in range(o_ref.shape[0]):
            o_ref[blk, block_rows:, :] = jnp.zeros((pad, LAGS), jnp.float32)
    for u in range(group):
        cc = trace_corr(src_ref[u], p_ref, u, rows, win) * scale
        first = u * rows
        while first < (u + 1) * rows:
            blk, at = divmod(first, block_rows)
            take = min(block_rows - at, (u + 1) * rows - first)
            o_ref[blk, at: at + take, :] = cc[first - u * rows: first - u * rows + take]
            first += take
    even_core = core_ref[0] == 0
    for half in range(kept_ref.shape[0]):
        even, odd = o_ref[2 * half], o_ref[2 * half + 1]
        kept_ref[half] = jnp.where(even_core, even, odd)
        sent_ref[half] = jnp.where(even_core, odd, even)


def correlate(core, src, partner_rows, scale, block_rows):
    traces, rows, win = partner_rows.shape
    span = src.shape[-1]
    group = block_rows // math.gcd(block_rows, rows)
    blocks = group * rows // block_rows
    if blocks % 2:
        group, blocks = 2 * group, 2 * blocks
    padded = -(-block_rows // 8) * 8
    flops = 2 * traces * rows * win * LAGS
    half_shape = jax.ShapeDtypeStruct((traces * rows // block_rows // 2, padded, LAGS), jnp.float32)
    out_spec = pl.BlockSpec((blocks // 2, padded, LAGS), lambda g, c: (g, 0, 0))
    return pl.pallas_call(
        lambda c, s, p, k, o, w: corr_kernel(c, s, p, k, o, w, win=win, scale=scale, block_rows=block_rows),
        grid_spec=pltpu.PrefetchScalarGridSpec(
            num_scalar_prefetch=1,
            grid=(traces // group,),
            in_specs=[
                pl.BlockSpec((group, 1, span), lambda g, c: (g, 0, 0)),
                pl.BlockSpec((group, rows, win), lambda g, c: (g, 0, 0)),
            ],
            out_specs=[out_spec, out_spec],
            scratch_shapes=[pltpu.VMEM((blocks, padded, LAGS), jnp.float32)],
        ),
        out_shape=[half_shape, half_shape],
        cost_estimate=pl.CostEstimate(
            flops=flops, transcendentals=0,
            bytes_accessed=traces * (rows * win * 2 + span * 4 + rows * LAGS * 4),
        ),
        name="xcorr",
    )(core.reshape(1), src.reshape(traces, 1, span), partner_rows)


def shards(record, requested, partners, codes, counts):
    whitened = normalize(record)
    local_stations, comp_count, window_count, window_len = whitened.shape
    owners = lax.axis_size("pairs")
    chips = lax.axis_size("z")
    cores = lax.axis_size("c")
    tm_count = chips * cores
    capacity = requested.shape[2]
    per_trace = partners.shape[2]
    trace_count = local_stations * comp_count
    own_index = lax.axis_index("pairs")
    per_station = comp_count * window_count * window_len
    mine = flip_lanes(whitened).reshape(local_stations, 8, per_station // 8)
    asked_of_me = lax.dynamic_index_in_dim(requested, own_index, axis=1, keepdims=False)
    pick_send = (asked_of_me[:, :, None] == jnp.arange(local_stations, dtype=jnp.int32)[None, None, :])
    outgoing = jnp.einsum("eis,sru->eiru", pick_send.astype(jnp.bfloat16), mine,
                          preferred_element_type=jnp.float32)
    outgoing = outgoing.astype(jnp.bfloat16).reshape(owners, capacity * 8, per_station // 8)
    arrived = lax.all_to_all(outgoing, "pairs", 0, 0, tiled=True)
    trace_pool = arrived.reshape(owners * capacity * comp_count, window_count * window_len)
    row_ids = (partners[0] * comp_count + codes[0]).reshape(-1)
    live_rows = (jnp.arange(per_trace, dtype=jnp.int32)[None, :] < counts[0][:, None]).reshape(-1)
    pool_rows = owners * capacity * comp_count
    pick_recv = (row_ids[:, None] == jnp.arange(pool_rows, dtype=jnp.int32)[None, :]) & live_rows[:, None]
    picked = jnp.dot(pick_recv.astype(jnp.bfloat16), trace_pool, preferred_element_type=jnp.float32)
    picked = picked.astype(jnp.bfloat16).reshape(trace_count, per_trace, window_len)
    half = LAGS // 2
    own = whitened.reshape(trace_count, window_len).astype(jnp.float32)
    span = ((window_len + LAGS + LANE - 1) // LANE) * LANE
    src = jnp.pad(own, ((0, 0), (half, span - window_len - half)))
    total_windows = window_count * tm_count
    scale = 1.0 / math.sqrt(window_len * total_windows)
    block_rows = trace_count * per_trace // tm_count
    core = lax.axis_index("c").astype(jnp.int32)
    kept, given = correlate(core, src, picked, scale, block_rows)
    got = lax.ppermute(given, "c", [(0, 1), (1, 0)])
    chip_sums = (kept + got)[:, :block_rows].astype(jnp.bfloat16).reshape(chips, 32, block_rows * LAGS // 32)
    arrived_sums = lax.all_to_all(chip_sums, "z", 0, 0, tiled=True)
    total = jnp.sum(arrived_sums.astype(jnp.float32), axis=0)
    return total.reshape(1, block_rows, LAGS)


def solution(mesh):
    tm_count = mesh.shape["tm"]
    split = jax.sharding.Mesh(
        mesh.devices.reshape(tm_count // 2, 2, mesh.shape["pairs"]), ("z", "c", "pairs")
    )
    tm = ("z", "c")
    return jax.shard_map(
        shards,
        mesh=split,
        in_specs=(
            P("pairs", None, tm, None),
            P(),
            P("pairs", None, None),
            P("pairs", None, None),
            P("pairs", None),
        ),
        out_specs=P("pairs", tm, None),
        check_vma=False,
    )
```

```python
import math

import jax
import jax.numpy as jnp
from jax import lax
from jax.experimental import pallas as pl
from jax.experimental.pallas import tpu as pltpu
from jax.sharding import PartitionSpec as P

LAGS = 1024
BLK = 256
LANE = 128


def normalize(traces):
    values = traces.astype(jnp.float32)
    values = values - jnp.mean(values, axis=-1, keepdims=True)
    power_mean = jnp.mean(values * values, axis=-1, keepdims=True)
    return (values * lax.rsqrt(power_mean + 1e-06)).astype(jnp.bfloat16)


def flip_lanes(rows):
    shape = rows.shape
    grouped = rows.reshape(shape[:-1] + (shape[-1] // LANE, LANE))
    return grouped[..., ::-1].reshape(shape)


def trace_corr(src_row, p_ref, u, rows, win):
    span = src_row.shape[1]
    m_blocks = win // BLK
    o_blocks = LAGS // BLK
    d_blocks = m_blocks + o_blocks - 1
    width = BLK * (d_blocks - 1) + BLK + LANE
    wide = jnp.broadcast_to(src_row, (LANE, span))
    hank = pltpu.roll(wide, span - (LANE - 1), 1, stride=1, stride_axis=0)
    hank = hank[:, :width].astype(jnp.bfloat16)
    acc = [jnp.zeros((rows, BLK), jnp.float32) for _ in range(o_blocks)]
    for d in range(d_blocks):
        rhs = jnp.concatenate(
            [hank[:, BLK * d: BLK * d + BLK], hank[:, BLK * d + LANE: BLK * d + LANE + BLK]], axis=0
        )
        lags = [o for o in range(o_blocks) if 0 <= d - o < m_blocks]
        lhs = jnp.concatenate([p_ref[u, :, BLK * (d - o): BLK * (d - o) + BLK] for o in lags], axis=0)
        res = jnp.dot(lhs, rhs, preferred_element_type=jnp.float32)
        for k, o in enumerate(lags):
            acc[o] = acc[o] + res[rows * k: rows * (k + 1)]
    return jnp.concatenate(acc, axis=1)


def corr_kernel(core_ref, src_ref, p_ref, kept_ref, sent_ref, o_ref, *, win, scale, block_rows):
    group, rows = p_ref.shape[0], p_ref.shape[1]
    pad = o_ref.shape[1] - block_rows
    if pad:
        for blk in range(o_ref.shape[0]):
            o_ref[blk, block_rows:, :] = jnp.zeros((pad, LAGS), jnp.float32)
    for u in range(group):
        cc = trace_corr(src_ref[u], p_ref, u, rows, win) * scale
        first = u * rows
        while first < (u + 1) * rows:
            blk, at = divmod(first, block_rows)
            take = min(block_rows - at, (u + 1) * rows - first)
            o_ref[blk, at: at + take, :] = cc[first - u * rows: first - u * rows + take]
            first += take
    even_core = core_ref[0] == 0
    for half in range(kept_ref.shape[0]):
        even, odd = o_ref[2 * half], o_ref[2 * half + 1]
        kept_ref[half] = jnp.where(even_core, even, odd)
        sent_ref[half] = jnp.where(even_core, odd, even)


def correlate(core, src, partner_rows, scale, block_rows):
    traces, rows, win = partner_rows.shape
    span = src.shape[-1]
    group = block_rows // math.gcd(block_rows, rows)
    blocks = group * rows // block_rows
    if blocks % 2:
        group, blocks = 2 * group, 2 * blocks
    padded = block_rows
    flops = 2 * traces * rows * win * LAGS
    half_shape = jax.ShapeDtypeStruct((traces * rows // block_rows // 2, padded, LAGS), jnp.float32)
    out_spec = pl.BlockSpec((blocks // 2, padded, LAGS), lambda g, c: (g, 0, 0))
    return pl.pallas_call(
        lambda c, s, p, k, o, w: corr_kernel(c, s, p, k, o, w, win=win, scale=scale, block_rows=block_rows),
        grid_spec=pltpu.PrefetchScalarGridSpec(
            num_scalar_prefetch=1,
            grid=(traces // group,),
            in_specs=[
                pl.BlockSpec((group, 1, span), lambda g, c: (g, 0, 0)),
                pl.BlockSpec((group, rows, win), lambda g, c: (g, 0, 0)),
            ],
            out_specs=[out_spec, out_spec],
            scratch_shapes=[pltpu.VMEM((blocks, padded, LAGS), jnp.float32)],
        ),
        out_shape=[half_shape, half_shape],
        cost_estimate=pl.CostEstimate(
            flops=flops, transcendentals=0,
            bytes_accessed=traces * (rows * win * 2 + span * 4 + rows * LAGS * 4),
        ),
        name="xcorr",
    )(core.reshape(1), src.reshape(traces, 1, span), partner_rows)


def shards(record, requested, partners, codes, counts):
    whitened = normalize(record)
    local_stations, comp_count, window_count, window_len = whitened.shape
    owners = lax.axis_size("pairs")
    chips = lax.axis_size("z")
    cores = lax.axis_size("c")
    tm_count = chips * cores
    capacity = requested.shape[2]
    per_trace = partners.shape[2]
    trace_count = local_stations * comp_count
    own_index = lax.axis_index("pairs")
    per_station = comp_count * window_count * window_len
    mine = flip_lanes(whitened).reshape(local_stations, 8, per_station // 8)
    asked_of_me = lax.dynamic_index_in_dim(requested, own_index, axis=1, keepdims=False)
    pick_send = (asked_of_me[:, :, None] == jnp.arange(local_stations, dtype=jnp.int32)[None, None, :])
    outgoing = jnp.einsum("eis,sru->eiru", pick_send.astype(jnp.bfloat16), mine,
                          preferred_element_type=jnp.float32)
    outgoing = outgoing.astype(jnp.bfloat16).reshape(owners, capacity * 8, per_station // 8)
    arrived = lax.all_to_all(outgoing, "pairs", 0, 0, tiled=True)
    trace_pool = arrived.reshape(owners * capacity * comp_count, window_count * window_len)
    row_ids = (partners[0] * comp_count + codes[0]).reshape(-1)
    live_rows = (jnp.arange(per_trace, dtype=jnp.int32)[None, :] < counts[0][:, None]).reshape(-1)
    pool_rows = owners * capacity * comp_count
    pick_recv = (row_ids[:, None] == jnp.arange(pool_rows, dtype=jnp.int32)[None, :]) & live_rows[:, None]
    picked = jnp.dot(pick_recv.astype(jnp.bfloat16), trace_pool, preferred_element_type=jnp.float32)
    picked = picked.astype(jnp.bfloat16).reshape(trace_count, per_trace, window_len)
    half = LAGS // 2
    own = whitened.reshape(trace_count, window_len).astype(jnp.float32)
    span = ((window_len + LAGS + LANE - 1) // LANE) * LANE
    src = jnp.pad(own, ((0, 0), (half, span - window_len - half)))
    total_windows = window_count * tm_count
    scale = 1.0 / math.sqrt(window_len * total_windows)
    block_rows = trace_count * per_trace // tm_count
    core = lax.axis_index("c").astype(jnp.int32)
    kept, given = correlate(core, src, picked, scale, block_rows)
    got = lax.ppermute(given, "c", [(0, 1), (1, 0)])
    chip_sums = (kept + got)[:, :block_rows].astype(jnp.bfloat16).reshape(chips, 32, block_rows * LAGS // 32)
    arrived_sums = lax.all_to_all(chip_sums, "z", 0, 0, tiled=True)
    total = jnp.sum(arrived_sums.astype(jnp.float32), axis=0)
    return total.reshape(1, block_rows, LAGS)


def solution(mesh):
    tm_count = mesh.shape["tm"]
    split = jax.sharding.Mesh(
        mesh.devices.reshape(tm_count // 2, 2, mesh.shape["pairs"]), ("z", "c", "pairs")
    )
    tm = ("z", "c")
    return jax.shard_map(
        shards,
        mesh=split,
        in_specs=(
            P("pairs", None, tm, None),
            P(),
            P("pairs", None, None),
            P("pairs", None, None),
            P("pairs", None),
        ),
        out_specs=P("pairs", tm, None),
        check_vma=False,
    )
```

```python
import math

import jax
import jax.numpy as jnp
from jax import lax
from jax.experimental import pallas as pl
from jax.experimental.pallas import tpu as pltpu
from jax.sharding import PartitionSpec as P

LAGS = 1024
BLK = 256
LANE = 128


def normalize(traces):
    values = traces.astype(jnp.float32)
    values = values - jnp.mean(values, axis=-1, keepdims=True)
    power_mean = jnp.mean(values * values, axis=-1, keepdims=True)
    return (values * lax.rsqrt(power_mean + 1e-06)).astype(jnp.bfloat16)


def flip_lanes(rows):
    shape = rows.shape
    grouped = rows.reshape(shape[:-1] + (shape[-1] // LANE, LANE))
    return grouped[..., ::-1].reshape(shape)


def trace_corr(src_row, p_ref, u, rows, win):
    span = src_row.shape[1]
    m_blocks = win // BLK
    o_blocks = LAGS // BLK
    d_blocks = m_blocks + o_blocks - 1
    width = BLK * (d_blocks - 1) + BLK + LANE
    wide = jnp.broadcast_to(src_row, (LANE, span))
    hank = pltpu.roll(wide, span - (LANE - 1), 1, stride=1, stride_axis=0)
    hank = hank[:, :width].astype(jnp.bfloat16)
    acc = [jnp.zeros((rows, BLK), jnp.float32) for _ in range(o_blocks)]
    for d in range(d_blocks):
        rhs = jnp.concatenate(
            [hank[:, BLK * d: BLK * d + BLK], hank[:, BLK * d + LANE: BLK * d + LANE + BLK]], axis=0
        )
        lags = [o for o in range(o_blocks) if 0 <= d - o < m_blocks]
        lhs = jnp.concatenate([p_ref[u, :, BLK * (d - o): BLK * (d - o) + BLK] for o in lags], axis=0)
        res = jnp.dot(lhs, rhs, preferred_element_type=jnp.float32)
        for k, o in enumerate(lags):
            acc[o] = acc[o] + res[rows * k: rows * (k + 1)]
    return jnp.concatenate(acc, axis=1)


def corr_kernel(core_ref, src_ref, p_ref, kept_ref, sent_ref, o_ref, *, win, scale, block_rows):
    group, rows = p_ref.shape[0], p_ref.shape[1]
    pad = o_ref.shape[1] - block_rows
    if pad:
        for blk in range(o_ref.shape[0]):
            o_ref[blk, block_rows:, :] = jnp.zeros((pad, LAGS), jnp.float32)
    for u in range(group):
        cc = trace_corr(src_ref[u], p_ref, u, rows, win) * scale
        first = u * rows
        while first < (u + 1) * rows:
            blk, at = divmod(first, block_rows)
            take = min(block_rows - at, (u + 1) * rows - first)
            o_ref[blk, at: at + take, :] = cc[first - u * rows: first - u * rows + take]
            first += take
    even_core = core_ref[0] == 0
    for half in range(kept_ref.shape[0]):
        even, odd = o_ref[2 * half], o_ref[2 * half + 1]
        kept_ref[half] = jnp.where(even_core, even, odd)
        sent_ref[half] = jnp.where(even_core, odd, even)


def correlate(core, src, partner_rows, scale, block_rows):
    traces, rows, win = partner_rows.shape
    span = src.shape[-1]
    group = block_rows // math.gcd(block_rows, rows)
    blocks = group * rows // block_rows
    if blocks % 2:
        group, blocks = 2 * group, 2 * blocks
    padded = -(-block_rows // 8) * 8
    flops = 2 * traces * rows * win * LAGS
    half_shape = jax.ShapeDtypeStruct((traces * rows // block_rows // 2, padded, LAGS), jnp.float32)
    out_spec = pl.BlockSpec((blocks // 2, padded, LAGS), lambda g, c: (g, 0, 0))
    return pl.pallas_call(
        lambda c, s, p, k, o, w: corr_kernel(c, s, p, k, o, w, win=win, scale=scale, block_rows=block_rows),
        grid_spec=pltpu.PrefetchScalarGridSpec(
            num_scalar_prefetch=1,
            grid=(traces // group,),
            in_specs=[
                pl.BlockSpec((group, 1, span), lambda g, c: (g, 0, 0)),
                pl.BlockSpec((group, rows, win), lambda g, c: (g, 0, 0)),
            ],
            out_specs=[out_spec, out_spec],
            scratch_shapes=[pltpu.VMEM((blocks, padded, LAGS), jnp.float32)],
        ),
        out_shape=[half_shape, half_shape],
        cost_estimate=pl.CostEstimate(
            flops=flops, transcendentals=0,
            bytes_accessed=traces * (rows * win * 2 + span * 4 + rows * LAGS * 4),
        ),
        name="xcorr",
    )(core.reshape(1), src.reshape(traces, 1, span), partner_rows)


def shards(record, requested, partners, codes, counts):
    whitened = normalize(record)
    local_stations, comp_count, window_count, window_len = whitened.shape
    owners = lax.axis_size("pairs")
    chips = lax.axis_size("z")
    cores = lax.axis_size("c")
    tm_count = chips * cores
    capacity = requested.shape[2]
    per_trace = partners.shape[2]
    trace_count = local_stations * comp_count
    own_index = lax.axis_index("pairs")
    per_station = comp_count * window_count * window_len
    mine = flip_lanes(whitened).reshape(local_stations, 8, per_station // 8)
    asked_of_me = lax.dynamic_index_in_dim(requested, own_index, axis=1, keepdims=False)
    pick_send = (asked_of_me[:, :, None] == jnp.arange(local_stations, dtype=jnp.int32)[None, None, :])
    outgoing = jnp.einsum("eis,sru->eiru", pick_send.astype(jnp.bfloat16), mine,
                          preferred_element_type=jnp.float32)
    outgoing = outgoing.astype(jnp.bfloat16).reshape(owners, capacity * 8, per_station // 8)
    arrived = lax.all_to_all(outgoing, "pairs", 0, 0, tiled=True)
    trace_pool = arrived.reshape(owners * capacity * comp_count, window_count * window_len)
    row_ids = (partners[0] * comp_count + codes[0]).reshape(-1)
    live_rows = (jnp.arange(per_trace, dtype=jnp.int32)[None, :] < counts[0][:, None]).reshape(-1)
    pool_rows = owners * capacity * comp_count
    pick_recv = (row_ids[:, None] == jnp.arange(pool_rows, dtype=jnp.int32)[None, :]) & live_rows[:, None]
    pick_recv = pick_recv.astype(jnp.bfloat16).reshape(2, trace_count // 2 * per_trace, pool_rows)
    half = LAGS // 2
    own = whitened.reshape(trace_count, window_len).astype(jnp.float32)
    span = ((window_len + LAGS + LANE - 1) // LANE) * LANE
    src = jnp.pad(own, ((0, 0), (half, span - window_len - half)))
    total_windows = window_count * tm_count
    scale = 1.0 / math.sqrt(window_len * total_windows)
    block_rows = trace_count * per_trace // tm_count
    core = lax.axis_index("c").astype(jnp.int32)
    sums = []
    for part in range(2):
        picked = jnp.dot(pick_recv[part], trace_pool, preferred_element_type=jnp.float32)
        picked = picked.astype(jnp.bfloat16).reshape(trace_count // 2, per_trace, window_len)
        own_part = src[part * trace_count // 2: (part + 1) * trace_count // 2]
        kept, given = correlate(core, own_part, picked, scale, block_rows)
        got = lax.ppermute(given, "c", [(0, 1), (1, 0)])
        sums.append(kept + got)
    chip_sums = jnp.concatenate(sums, axis=0)
    chip_sums = chip_sums[:, :block_rows].astype(jnp.bfloat16).reshape(chips, 32, block_rows * LAGS // 32)
    arrived_sums = lax.all_to_all(chip_sums, "z", 0, 0, tiled=True)
    total = jnp.sum(arrived_sums.astype(jnp.float32), axis=0)
    return total.reshape(1, block_rows, LAGS)


def solution(mesh):
    tm_count = mesh.shape["tm"]
    split = jax.sharding.Mesh(
        mesh.devices.reshape(tm_count // 2, 2, mesh.shape["pairs"]), ("z", "c", "pairs")
    )
    tm = ("z", "c")
    return jax.shard_map(
        shards,
        mesh=split,
        in_specs=(
            P("pairs", None, tm, None),
            P(),
            P("pairs", None, None),
            P("pairs", None, None),
            P("pairs", None),
        ),
        out_specs=P("pairs", tm, None),
        check_vma=False,
    )
```

```python
import math

import jax
import jax.numpy as jnp
from jax import lax
from jax.experimental import pallas as pl
from jax.experimental.pallas import tpu as pltpu
from jax.sharding import PartitionSpec as P

LAGS = 1024
BLK = 256
LANE = 128


def normalize(traces):
    values = traces.astype(jnp.float32)
    values = values - jnp.mean(values, axis=-1, keepdims=True)
    power_mean = jnp.mean(values * values, axis=-1, keepdims=True)
    return (values * lax.rsqrt(power_mean + 1e-06)).astype(jnp.bfloat16)


def flip_lanes(rows):
    shape = rows.shape
    grouped = rows.reshape(shape[:-1] + (shape[-1] // LANE, LANE))
    return grouped[..., ::-1].reshape(shape)


def trace_corr(src_row, p_ref, u, rows, win):
    span = src_row.shape[1]
    m_blocks = win // BLK
    o_blocks = LAGS // BLK
    d_blocks = m_blocks + o_blocks - 1
    width = BLK * (d_blocks - 1) + BLK + LANE
    wide = jnp.broadcast_to(src_row, (LANE, span))
    hank = pltpu.roll(wide, span - (LANE - 1), 1, stride=1, stride_axis=0)
    hank = hank[:, :width].astype(jnp.bfloat16)
    acc = [jnp.zeros((rows, BLK), jnp.float32) for _ in range(o_blocks)]
    for d in range(d_blocks):
        rhs = jnp.concatenate(
            [hank[:, BLK * d: BLK * d + BLK], hank[:, BLK * d + LANE: BLK * d + LANE + BLK]], axis=0
        )
        lags = [o for o in range(o_blocks) if 0 <= d - o < m_blocks]
        lhs = jnp.concatenate([p_ref[u, :, BLK * (d - o): BLK * (d - o) + BLK] for o in lags], axis=0)
        res = jnp.dot(lhs, rhs, preferred_element_type=jnp.float32)
        for k, o in enumerate(lags):
            acc[o] = acc[o] + res[rows * k: rows * (k + 1)]
    return jnp.concatenate(acc, axis=1)


def corr_kernel(core_ref, src_ref, p_ref, kept_ref, sent_ref, o_ref, *, win, scale, block_rows):
    group, rows = p_ref.shape[0], p_ref.shape[1]
    pad = o_ref.shape[1] - block_rows
    if pad:
        for blk in range(o_ref.shape[0]):
            o_ref[blk, block_rows:, :] = jnp.zeros((pad, LAGS), jnp.float32)
    for u in range(group):
        cc = trace_corr(src_ref[u], p_ref, u, rows, win) * scale
        first = u * rows
        while first < (u + 1) * rows:
            blk, at = divmod(first, block_rows)
            take = min(block_rows - at, (u + 1) * rows - first)
            o_ref[blk, at: at + take, :] = cc[first - u * rows: first - u * rows + take]
            first += take
    even_core = core_ref[0] == 0
    for half in range(kept_ref.shape[0]):
        even, odd = o_ref[2 * half], o_ref[2 * half + 1]
        kept_ref[half] = jnp.where(even_core, even, odd)
        sent_ref[half] = jnp.where(even_core, odd, even)


def correlate(core, src, partner_rows, scale, block_rows):
    traces, rows, win = partner_rows.shape
    span = src.shape[-1]
    group = block_rows // math.gcd(block_rows, rows)
    blocks = group * rows // block_rows
    if blocks % 2:
        group, blocks = 2 * group, 2 * blocks
    padded = -(-block_rows // 8) * 8
    flops = 2 * traces * rows * win * LAGS
    half_shape = jax.ShapeDtypeStruct((traces * rows // block_rows // 2, padded, LAGS), jnp.float32)
    out_spec = pl.BlockSpec((blocks // 2, padded, LAGS), lambda g, c: (g, 0, 0))
    return pl.pallas_call(
        lambda c, s, p, k, o, w: corr_kernel(c, s, p, k, o, w, win=win, scale=scale, block_rows=block_rows),
        grid_spec=pltpu.PrefetchScalarGridSpec(
            num_scalar_prefetch=1,
            grid=(traces // group,),
            in_specs=[
                pl.BlockSpec((group, 1, span), lambda g, c: (g, 0, 0)),
                pl.BlockSpec((group, rows, win), lambda g, c: (g, 0, 0)),
            ],
            out_specs=[out_spec, out_spec],
            scratch_shapes=[pltpu.VMEM((blocks, padded, LAGS), jnp.float32)],
        ),
        out_shape=[half_shape, half_shape],
        cost_estimate=pl.CostEstimate(
            flops=flops, transcendentals=0,
            bytes_accessed=traces * (rows * win * 2 + span * 4 + rows * LAGS * 4),
        ),
        name="xcorr",
    )(core.reshape(1), src.reshape(traces, 1, span), partner_rows)


def shards(record, requested, partners, codes, counts):
    whitened = normalize(record)
    local_stations, comp_count, window_count, window_len = whitened.shape
    owners = lax.axis_size("pairs")
    chips = lax.axis_size("z")
    cores = lax.axis_size("c")
    tm_count = chips * cores
    capacity = requested.shape[2]
    per_trace = partners.shape[2]
    trace_count = local_stations * comp_count
    own_index = lax.axis_index("pairs")
    per_station = comp_count * window_count * window_len
    mine = flip_lanes(whitened).reshape(local_stations, 8, per_station // 8)
    asked_of_me = lax.dynamic_index_in_dim(requested, own_index, axis=1, keepdims=False)
    pick_send = (asked_of_me[:, :, None] == jnp.arange(local_stations, dtype=jnp.int32)[None, None, :])
    outgoing = jnp.einsum("eis,sru->eiru", pick_send.astype(jnp.bfloat16), mine,
                          preferred_element_type=jnp.bfloat16)
    outgoing = outgoing.reshape(owners, capacity * 8, per_station // 8)
    arrived = lax.all_to_all(outgoing, "pairs", 0, 0, tiled=True)
    trace_pool = arrived.reshape(owners * capacity * comp_count, window_count * window_len)
    row_ids = (partners[0] * comp_count + codes[0]).reshape(-1)
    live_rows = (jnp.arange(per_trace, dtype=jnp.int32)[None, :] < counts[0][:, None]).reshape(-1)
    pool_rows = owners * capacity * comp_count
    pick_recv = (row_ids[:, None] == jnp.arange(pool_rows, dtype=jnp.int32)[None, :]) & live_rows[:, None]
    picked = jnp.dot(pick_recv.astype(jnp.bfloat16), trace_pool, preferred_element_type=jnp.bfloat16)
    picked = picked.reshape(trace_count, per_trace, window_len)
    half = LAGS // 2
    own = whitened.reshape(trace_count, window_len).astype(jnp.float32)
    span = ((window_len + LAGS + LANE - 1) // LANE) * LANE
    src = jnp.pad(own, ((0, 0), (half, span - window_len - half)))
    total_windows = window_count * tm_count
    scale = 1.0 / math.sqrt(window_len * total_windows)
    block_rows = trace_count * per_trace // tm_count
    core = lax.axis_index("c").astype(jnp.int32)
    kept, given = correlate(core, src, picked, scale, block_rows)
    got = lax.ppermute(given, "c", [(0, 1), (1, 0)])
    chip_sums = (kept + got)[:, :block_rows].astype(jnp.bfloat16).reshape(chips, 32, block_rows * LAGS // 32)
    arrived_sums = lax.all_to_all(chip_sums, "z", 0, 0, tiled=True)
    total = jnp.sum(arrived_sums.astype(jnp.float32), axis=0)
    return total.reshape(1, block_rows, LAGS)


def solution(mesh):
    tm_count = mesh.shape["tm"]
    split = jax.sharding.Mesh(
        mesh.devices.reshape(tm_count // 2, 2, mesh.shape["pairs"]), ("z", "c", "pairs")
    )
    tm = ("z", "c")
    return jax.shard_map(
        shards,
        mesh=split,
        in_specs=(
            P("pairs", None, tm, None),
            P(),
            P("pairs", None, None),
            P("pairs", None, None),
            P("pairs", None),
        ),
        out_specs=P("pairs", tm, None),
        check_vma=False,
    )
```
